256 devices in a mesh: row: 2 (over core), col: 2 (over x_lo), rhs: 64 (over z, y, x_hi).
Axes of the slice: x: 4 (x_hi: 2, x_lo: 2; x = x_hi * 2 + x_lo), y: 4, z: 8, core: 2. Of those that a mesh axis runs over, the one named last changes fastest.
Arguments:
- front: bfloat16 [4096, 4096], P(('row', 'rhs'), 'col'), as said below
- anc_weight: bfloat16 [1024, 4096], P(('row', 'rhs'), 'col'), may hold values from -0.1875 to 0.1875
- solved: bfloat16 [2048, 8192], P(('row', 'col'), 'rhs'), may hold values from -6 to 6
- owners: int32 [8], replicated, may hold values from 0 to 3, as said below
- indices: int32 [8, 128], replicated, may hold values from 0 to 511
- counts: int32 [8], replicated, may hold values from 64 to 128, as said below
- rhs_side: bfloat16 [4096, 8192], P('row', 'rhs'), may hold values from -6 to 6
Outputs:
- solution: bfloat16 [4096, 8192], P('row', 'rhs')
The draws below stay inside these ranges and needn't reach their ends.
Inputs may be any that keep to these rules, and one draw needn't show every extreme that they name: `front`: zero above the diagonal; diagonal entries 1 or more. The 4 tiles of each aligned block of 4 tiles have 4 different owners, numbered row index times 2 plus col index. `counts`: rows at or past a tile's count are padding.
All inputs are finite; a program needn't handle non-finite values.
Results may differ from the reference program's by a relative error of at most 0.0038.
Values may be sent and summed in bfloat16 or wider, within the bound.
No kernel may reach another device: no remote copies, remote signals or barrier semaphores. Data moves between devices by JAX's collectives and lax.ppermute only.
A program may use at most 128 MiB of HBM per device.

```python
import math
import jax
import jax.numpy as jnp
from jax import lax

FRONT = 4096
TILE = 128
SRC_DEV = 512
NTB = 4
ANC = 1024
NTILES = 8
RHS = 8192
N_ROW = 2
N_COL = 2


def draw_front(key, part):
    key_one, key_two = jax.random.split(key)
    row_ids = lax.broadcasted_iota(jnp.int32, (FRONT, FRONT), 0)
    col_ids = lax.broadcasted_iota(jnp.int32, (FRONT, FRONT), 1)
    spread = 0.6 / math.sqrt(FRONT)
    lower_part = jax.random.normal(key_one, (FRONT, FRONT), jnp.float32) * spread
    diagonal = jax.random.uniform(key_two, (FRONT, FRONT), jnp.float32, 1.0, 2.0)
    zeros_part = jnp.zeros((FRONT, FRONT), jnp.float32)
    result = jnp.where(row_ids > col_ids, lower_part, jnp.where(row_ids == col_ids, diagonal, zeros_part))
    return result.astype(jnp.bfloat16)


def draw_owners(key, part):
    key_list = jax.random.split(jax.random.fold_in(key, 11), N_ROW)
    orders = [jax.random.permutation(key_list[number], NTB) for number in range(N_ROW)]
    return jnp.concatenate(orders).astype(jnp.int32)


def draw_counts(key, part):
    key_one, key_two, key_three = jax.random.split(jax.random.fold_in(key, 23), 3)
    values = jax.random.randint(key_one, (NTILES,), 64, TILE + 1).astype(jnp.int32)
    first_pick = jax.random.randint(key_two, (), 0, NTILES).astype(jnp.int32)
    second_pick = (first_pick + 1 + jax.random.randint(key_three, (), 0, NTILES - 1).astype(jnp.int32)) % NTILES
    tile_ids = jnp.arange(NTILES, dtype=jnp.int32)
    values = jnp.where(tile_ids == first_pick, TILE, values)
    values = jnp.where(tile_ids == second_pick, 64, values)
    return values.astype(jnp.int32)


def touch_ends(values, key, smallest, high):
    longest = values.shape.index(max(values.shape))
    spots = []
    for shift in (0, 1):
        where = [jax.random.randint(jax.random.fold_in(key, axis), (), 0, length) for axis, length in enumerate(values.shape)]
        where[longest] = (where[longest] + shift) % values.shape[longest]
        spots.append(tuple(where))
    return values.at[spots[0]].set(smallest).at[spots[1]].set(high)


def steps_of(stream_key, shape, cuts, least, high):
    def one(dim, shards_of):
        heights = jax.random.uniform(jax.random.fold_in(jax.random.fold_in(stream_key, 6), dim), (shards_of,), jnp.float32, least / len(cuts), high / len(cuts))
        return jnp.repeat(jnp.exp(heights), shape[dim] // shards_of).reshape((-1,) + (1,) * (len(shape) - dim - 1))

    gain = one(*cuts[0])
    for cut in cuts[1:]:
        gain = gain * one(*cut)
    return gain


def normal_values(stream_key, shape, scale, limit, shards=(), held_as=jnp.bfloat16):
    values = jax.random.normal(stream_key, shape, jnp.float32) * scale
    if len(shards) > 0:
        values = steps_of(stream_key, shape, shards, -0.22, 0.18) * values
    return jnp.clip(values, min=-limit, max=limit).astype(held_as)


def setup_inputs(seed: int = 0) -> dict:
    splits = jax.random.split(jax.random.key(seed), 8)
    return {
        "front": draw_front(jax.random.fold_in(splits[7], 71), 0),
        "anc_weight": normal_values(splits[1], (ANC, FRONT), ANC ** -0.5, 0.1875, ((0, 128), (1, 2))),
        "solved": normal_values(splits[2], (SRC_DEV * N_ROW * N_COL, RHS), 1.0, 6.0, ((0, 4), (1, 64))),
        "owners": draw_owners(jax.random.fold_in(splits[7], 71), 0),
        "indices": touch_ends(jax.random.randint(splits[4], (NTILES, TILE), 0, SRC_DEV), jax.random.fold_in(splits[4], 1), 0, SRC_DEV - 1).astype(jnp.int32),
        "counts": draw_counts(jax.random.fold_in(splits[7], 71), 0),
        "rhs_side": normal_values(splits[6], (FRONT, RHS), 1.0, 6.0, ((0, 2), (1, 64))),
    }


def reference(front, anc_weight, solved, owners, indices, counts, rhs_side):
    blocks = N_ROW
    width = FRONT // blocks
    anc_rows = ANC // blocks
    source_rows = (owners[:, None] * SRC_DEV + indices).reshape(-1)
    live_rows = (jnp.arange(TILE, dtype=jnp.int32)[None, :] < counts[:, None]).reshape(-1)
    picked = solved[source_rows]
    ancestor_values = jnp.where(live_rows[:, None], picked, jnp.zeros_like(picked))
    anc_terms = []
    for block_b in range(blocks):
        weight_rows = anc_weight[block_b * anc_rows:(block_b + 1) * anc_rows].astype(jnp.float32)
        values_rows = ancestor_values[block_b * anc_rows:(block_b + 1) * anc_rows].astype(jnp.float32)
        anc_terms.append(jnp.dot(weight_rows.T.astype(jnp.float32), values_rows.astype(jnp.float32), precision=lax.Precision.HIGHEST, preferred_element_type=jnp.float32))
    solution_blocks = [None] * blocks
    for block_c in reversed(range(blocks)):
        cols = slice(block_c * width, (block_c + 1) * width)
        summed = jnp.zeros((width, rhs_side.shape[1]), jnp.float32)
        for block_b in range(blocks):
            term = anc_terms[block_b][cols]
            if block_b > block_c:
                tile_part = front[block_b * width:(block_b + 1) * width, cols].astype(jnp.float32)
                term = term + jnp.dot(tile_part.T.astype(jnp.float32), solution_blocks[block_b].astype(jnp.float32), precision=lax.Precision.HIGHEST, preferred_element_type=jnp.float32)
            rounded = lax.optimization_barrier(term.astype(jnp.bfloat16))
            summed = summed + rounded.astype(jnp.float32)
        reduced = rhs_side[cols].astype(jnp.float32) - summed
        diagonal = front[cols, cols].astype(jnp.float32)
        solved_block = jax.scipy.linalg.solve_triangular(diagonal, reduced, trans=1, lower=True)
        solution_blocks[block_c] = solved_block.astype(jnp.bfloat16)
    return jnp.concatenate(solution_blocks, axis=0)
```

```python
import jax
import jax.numpy as jnp
from jax import lax
from jax.sharding import PartitionSpec as P

BLOCK = 128
HIGH = lax.Precision.HIGHEST


def split_dot_t(mat_bf16, vec_f32):
    hi = vec_f32.astype(jnp.bfloat16)
    lo = (vec_f32 - hi.astype(jnp.float32)).astype(jnp.bfloat16)
    dims = (((0,), (0,)), ((), ()))
    out = lax.dot_general(mat_bf16, hi, dims, preferred_element_type=jnp.float32)
    return out + lax.dot_general(mat_bf16, lo, dims, preferred_element_type=jnp.float32)


def prepare(tile):
    n = tile.shape[0]
    nb = n // BLOCK
    blocks = jnp.stack(
        [tile[j * BLOCK:(j + 1) * BLOCK, j * BLOCK:(j + 1) * BLOCK] for j in range(nb)]
    ).astype(jnp.float32)
    eye = jnp.eye(BLOCK, dtype=jnp.float32)
    diag = jnp.sum(blocks * eye[None], axis=2)
    lower = jnp.tril(jnp.ones((BLOCK, BLOCK), jnp.bool_), -1)
    nil = jnp.where(lower[None], blocks / diag[:, :, None], 0.0)
    prod = eye[None] - nil
    power = nil
    steps = 1
    while 2 ** steps < BLOCK:
        power = jnp.einsum("bij,bjk->bik", power, power, precision=HIGH)
        prod = jnp.einsum("bij,bjk->bik", prod, eye[None] + power, precision=HIGH)
        steps += 1
    return prod, 1.0 / diag


def apply_solve(tile, prod, inv_diag, rhs):
    n = tile.shape[0]
    nb = n // BLOCK
    cols = rhs.shape[1]

    def body(i, carry):
        rest, out = carry
        j = nb - 1 - i
        r_j = lax.dynamic_slice_in_dim(rest, j * BLOCK, BLOCK, 0)
        p_j = lax.dynamic_index_in_dim(prod, j, 0, keepdims=False)
        d_j = lax.dynamic_index_in_dim(inv_diag, j, 0, keepdims=False)
        v_j = jnp.einsum("ji,jk->ik", p_j, r_j, precision=HIGH) * d_j[:, None]
        rows = lax.dynamic_slice_in_dim(tile, j * BLOCK, BLOCK, 0)
        rest = rest - split_dot_t(rows, v_j)
        out = lax.dynamic_update_slice_in_dim(out, v_j, j * BLOCK, 0)
        return rest, out

    _, out = lax.fori_loop(0, nb, body, (rhs, jnp.zeros((n, cols), jnp.float32)))
    return out


def on_device(front, anc_weight, solved, owners, indices, counts, rhs_side):
    row_count = lax.axis_size("row")
    col_count = lax.axis_size("col")
    tiles_block = row_count * col_count
    row_index = lax.axis_index("row")
    col_index = lax.axis_index("col")
    tile_rows = indices.shape[1]
    columns = solved.shape[1]
    self_id = row_index * col_count + col_index
    owner_grid = owners.reshape(row_count, tiles_block)
    mine = (owner_grid == self_id).astype(jnp.int32)
    position = jnp.sum(mine * jnp.arange(tiles_block, dtype=jnp.int32)[None, :], axis=1)
    tile_ids = jnp.arange(row_count, dtype=jnp.int32) * tiles_block + position
    local_rows = indices[tile_ids]
    live_rows = jnp.arange(tile_rows, dtype=jnp.int32)[None, :] < counts[tile_ids][:, None]
    picked = solved[local_rows.reshape(-1)].reshape(row_count, tile_rows, columns)
    picked = jnp.where(live_rows[:, :, None], picked, jnp.zeros_like(picked))
    block_owners = lax.dynamic_slice_in_dim(owners, row_index * tiles_block, tiles_block)
    outgoing = jnp.broadcast_to(picked[:, None], (row_count, col_count, tile_rows, columns))
    outgoing = outgoing.reshape(row_count * col_count * tile_rows, columns)
    received = lax.all_to_all(outgoing, ("row", "col"), split_axis=0, concat_axis=0, tiled=True)
    slot_rows = received.reshape(tiles_block, tile_rows, columns)
    anc_values = slot_rows[block_owners].reshape(tiles_block * tile_rows, columns)
    weight_tile = lax.all_gather(anc_weight, "rhs", axis=0, tiled=True)
    front_tile = lax.all_gather(front, "rhs", axis=0, tiled=True)
    width = front_tile.shape[1]
    anc_total = lax.dot_general(
        weight_tile, anc_values, (((0,), (0,)), ((), ())), preferred_element_type=jnp.float32
    )
    prod, inv_diag = prepare(front_tile)
    rhs_values = rhs_side.astype(jnp.float32)
    down = [(1, 0)]
    left = [(1, 0)]
    right = [(0, 1)]

    own_one = anc_total.astype(jnp.bfloat16)
    other_one = lax.ppermute(own_one, "row", [(0, 1)])
    reduced_one = rhs_values - own_one.astype(jnp.float32) - other_one.astype(jnp.float32)
    sol_one = apply_solve(front_tile, prod, inv_diag, reduced_one).astype(jnp.bfloat16)
    got_one = lax.ppermute(sol_one, "col", left)
    sol_one = jnp.where(col_index == 1, sol_one, got_one)

    own_zero = (anc_total + split_dot_t(front_tile, sol_one.astype(jnp.float32))).astype(jnp.bfloat16)
    own_zero = jnp.where(row_index == 0, anc_total.astype(jnp.bfloat16), own_zero)
    other_zero = lax.ppermute(own_zero, "row", down)
    reduced_zero = rhs_values - own_zero.astype(jnp.float32) - other_zero.astype(jnp.float32)
    sol_zero = apply_solve(front_tile, prod, inv_diag, reduced_zero).astype(jnp.bfloat16)
    got_zero = lax.ppermute(sol_zero, "col", right)
    sol_zero = jnp.where(col_index == 0, sol_zero, got_zero)
    return jnp.where(row_index == 1, sol_one, sol_zero)


def solution(mesh):
    placed = (
        P(("row", "rhs"), "col"),
        P(("row", "rhs"), "col"),
        P(("row", "col"), "rhs"),
        P(),
        P(),
        P(),
        P("row", "rhs"),
    )
    return jax.shard_map(
        on_device, mesh=mesh, in_specs=placed, out_specs=P("row", "rhs"), check_vma=False
    )
```

```python
import jax
import jax.numpy as jnp
from jax import lax
from jax.sharding import PartitionSpec as P

BLOCK = 128
HIGH = lax.Precision.HIGHEST


def split_dot_t(mat_bf16, vec_f32):
    hi = vec_f32.astype(jnp.bfloat16)
    lo = (vec_f32 - hi.astype(jnp.float32)).astype(jnp.bfloat16)
    dims = (((0,), (0,)), ((), ()))
    out = lax.dot_general(mat_bf16, hi, dims, preferred_element_type=jnp.float32)
    return out + lax.dot_general(mat_bf16, lo, dims, preferred_element_type=jnp.float32)


def prepare(tile):
    n = tile.shape[0]
    nb = n // BLOCK
    blocks = jnp.stack(
        [tile[j * BLOCK:(j + 1) * BLOCK, j * BLOCK:(j + 1) * BLOCK] for j in range(nb)]
    ).astype(jnp.float32)
    eye = jnp.eye(BLOCK, dtype=jnp.float32)
    diag = jnp.sum(blocks * eye[None], axis=2)
    lower = jnp.tril(jnp.ones((BLOCK, BLOCK), jnp.bool_), -1)
    nil = jnp.where(lower[None], blocks / diag[:, :, None], 0.0)
    prod = eye[None] - nil
    power = nil
    steps = 1
    while 2 ** steps < BLOCK:
        power = jnp.einsum("bij,bjk->bik", power, power, precision=HIGH)
        prod = jnp.einsum("bij,bjk->bik", prod, eye[None] + power, precision=HIGH)
        steps += 1
    return prod, 1.0 / diag


def apply_solve(tile, prod, inv_diag, rhs):
    n = tile.shape[0]
    nb = n // BLOCK
    cols = rhs.shape[1]

    def body(i, carry):
        rest, out = carry
        j = nb - 1 - i
        r_j = lax.dynamic_slice_in_dim(rest, j * BLOCK, BLOCK, 0)
        p_j = lax.dynamic_index_in_dim(prod, j, 0, keepdims=False)
        d_j = lax.dynamic_index_in_dim(inv_diag, j, 0, keepdims=False)
        v_j = jnp.einsum("ji,jk->ik", p_j, r_j, precision=HIGH) * d_j[:, None]
        rows = lax.dynamic_slice_in_dim(tile, j * BLOCK, BLOCK, 0)
        rest = rest - split_dot_t(rows, v_j)
        out = lax.dynamic_update_slice_in_dim(out, v_j, j * BLOCK, 0)
        return rest, out

    _, out = lax.fori_loop(0, nb, body, (rhs, jnp.zeros((n, cols), jnp.float32)))
    return out


def on_device(front, anc_weight, solved, owners, indices, counts, rhs_side):
    row_count = lax.axis_size("row")
    col_count = lax.axis_size("col")
    tiles_block = row_count * col_count
    row_index = lax.axis_index("row")
    col_index = lax.axis_index("col")
    tile_rows = indices.shape[1]
    columns = solved.shape[1]
    self_id = row_index * col_count + col_index
    owner_grid = owners.reshape(row_count, tiles_block)
    mine = (owner_grid == self_id).astype(jnp.int32)
    position = jnp.sum(mine * jnp.arange(tiles_block, dtype=jnp.int32)[None, :], axis=1)
    tile_ids = jnp.arange(row_count, dtype=jnp.int32) * tiles_block + position
    local_rows = indices[tile_ids]
    live_rows = jnp.arange(tile_rows, dtype=jnp.int32)[None, :] < counts[tile_ids][:, None]
    picked = solved[local_rows.reshape(-1)].reshape(row_count, tile_rows, columns)
    picked = jnp.where(live_rows[:, :, None], picked, jnp.zeros_like(picked))
    block_owners = lax.dynamic_slice_in_dim(owners, row_index * tiles_block, tiles_block)
    outgoing = jnp.broadcast_to(picked[:, None], (row_count, col_count, tile_rows, columns))
    outgoing = outgoing.reshape(row_count * col_count * tile_rows, columns)
    received = lax.all_to_all(outgoing, ("row", "col"), split_axis=0, concat_axis=0, tiled=True)
    slot_rows = received.reshape(tiles_block, tile_rows, columns)
    anc_values = slot_rows[block_owners].reshape(tiles_block * tile_rows, columns)
    w_rows = anc_weight.shape[0]
    both = jnp.concatenate([anc_weight, front], axis=0)
    for axis in ("xh", "y", "z"):
        both = lax.all_gather(both, axis, axis=0, tiled=True)
    both = both.reshape(-1, w_rows + front.shape[0], both.shape[1])
    weight_tile = both[:, :w_rows].reshape(-1, both.shape[2])
    front_tile = both[:, w_rows:].reshape(-1, both.shape[2])
    width = front_tile.shape[1]
    anc_total = lax.dot_general(
        weight_tile, anc_values, (((0,), (0,)), ((), ())), preferred_element_type=jnp.float32
    )
    prod, inv_diag = prepare(front_tile)
    rhs_values = rhs_side.astype(jnp.float32)
    down = [(1, 0)]
    left = [(1, 0)]
    right = [(0, 1)]

    own_one = anc_total.astype(jnp.bfloat16)
    other_one = lax.ppermute(own_one, "row", [(0, 1)])
    reduced_one = rhs_values - own_one.astype(jnp.float32) - other_one.astype(jnp.float32)
    sol_one = apply_solve(front_tile, prod, inv_diag, reduced_one).astype(jnp.bfloat16)
    got_one = lax.ppermute(sol_one, "col", left)
    sol_one = jnp.where(col_index == 1, sol_one, got_one)

    own_zero = (anc_total + split_dot_t(front_tile, sol_one.astype(jnp.float32))).astype(jnp.bfloat16)
    own_zero = jnp.where(row_index == 0, anc_total.astype(jnp.bfloat16), own_zero)
    other_zero = lax.ppermute(own_zero, "row", down)
    reduced_zero = rhs_values - own_zero.astype(jnp.float32) - other_zero.astype(jnp.float32)
    sol_zero = apply_solve(front_tile, prod, inv_diag, reduced_zero).astype(jnp.bfloat16)
    got_zero = lax.ppermute(sol_zero, "col", right)
    sol_zero = jnp.where(col_index == 0, sol_zero, got_zero)
    return jnp.where(row_index == 1, sol_one, sol_zero)


def solution(mesh):
    dims = dict(mesh.shape)
    rhs_split = (dims["rhs"] // 8, 4, 2)
    sub = jax.sharding.Mesh(
        mesh.devices.reshape(dims["row"], dims["col"], *rhs_split), ("row", "col", "z", "y", "xh")
    )
    rhs = ("z", "y", "xh")
    placed = (
        P(("row",) + rhs, "col"),
        P(("row",) + rhs, "col"),
        P(("row", "col"), rhs),
        P(),
        P(),
        P(),
        P("row", rhs),
    )
    return jax.shard_map(
        on_device, mesh=sub, in_specs=placed, out_specs=P("row", rhs), check_vma=False
    )
```

```python
import jax
import jax.numpy as jnp
from jax import lax
from jax.sharding import PartitionSpec as P
from jax.experimental import pallas as pl
from jax.experimental.pallas import tpu as pltpu

BLOCK = 128
HIGH = lax.Precision.HIGHEST


def split_dot_t(mat_bf16, vec_f32):
    hi = vec_f32.astype(jnp.bfloat16)
    lo = (vec_f32 - hi.astype(jnp.float32)).astype(jnp.bfloat16)
    dims = (((0,), (0,)), ((), ()))
    out = lax.dot_general(mat_bf16, hi, dims, preferred_element_type=jnp.float32)
    return out + lax.dot_general(mat_bf16, lo, dims, preferred_element_type=jnp.float32)


def prepare(tile):
    n = tile.shape[0]
    nb = n // BLOCK
    blocks = jnp.stack(
        [tile[j * BLOCK:(j + 1) * BLOCK, j * BLOCK:(j + 1) * BLOCK] for j in range(nb)]
    ).astype(jnp.float32)
    eye = jnp.eye(BLOCK, dtype=jnp.float32)
    diag = jnp.sum(blocks * eye[None], axis=2)
    lower = jnp.tril(jnp.ones((BLOCK, BLOCK), jnp.bool_), -1)
    nil = jnp.where(lower[None], blocks / diag[:, :, None], 0.0)
    prod = eye[None] - nil
    power = nil
    steps = 1
    while 2 ** steps < BLOCK:
        power = jnp.einsum("bij,bjk->bik", power, power, precision=HIGH)
        prod = jnp.einsum("bij,bjk->bik", prod, eye[None] + power, precision=HIGH)
        steps += 1
    return prod, 1.0 / diag


def split_bf16(x):
    hi = x.astype(jnp.bfloat16)
    return hi, (x - hi.astype(jnp.float32)).astype(jnp.bfloat16)


def solve_kernel(f_ref, p_ref, d_ref, r_ref, o_ref, rest_ref):
    nb = p_ref.shape[0]
    rest_ref[...] = r_ref[...]

    def body(i, carry):
        j = nb - 1 - i
        start = pl.multiple_of(j * BLOCK, BLOCK)
        r_hi, r_lo = split_bf16(rest_ref[:, pl.ds(start, BLOCK)])
        p_hi, p_lo = split_bf16(p_ref[j])
        v = jnp.dot(r_hi, p_hi, preferred_element_type=jnp.float32)
        v = v + jnp.dot(r_lo, p_hi, preferred_element_type=jnp.float32)
        v = v + jnp.dot(r_hi, p_lo, preferred_element_type=jnp.float32)
        v = v * d_ref[pl.ds(j, 1), :]
        v_hi, v_lo = split_bf16(v)
        rows = f_ref[pl.ds(start, BLOCK), :]
        upd = jnp.dot(v_hi, rows, preferred_element_type=jnp.float32)
        upd = upd + jnp.dot(v_lo, rows, preferred_element_type=jnp.float32)
        rest_ref[...] = rest_ref[...] - upd
        o_ref[:, pl.ds(start, BLOCK)] = v.astype(o_ref.dtype)
        return carry

    lax.fori_loop(0, nb, body, 0)


def kernel_solve(tile, prod, inv_diag, rhs):
    n = tile.shape[0]
    cols = rhs.shape[1]
    vmem = pl.BlockSpec(memory_space=pltpu.VMEM)
    out_t = pl.pallas_call(
        solve_kernel,
        out_shape=jax.ShapeDtypeStruct((cols, n), jnp.bfloat16),
        in_specs=[vmem, vmem, vmem, vmem],
        out_specs=vmem,
        scratch_shapes=[pltpu.VMEM((cols, n), jnp.float32)],
        compiler_params=pltpu.CompilerParams(vmem_limit_bytes=48 * 1024 * 1024),
    )(tile, prod, inv_diag, rhs.T)
    return out_t.T


def apply_solve(tile, prod, inv_diag, rhs):
    n = tile.shape[0]
    nb = n // BLOCK
    cols = rhs.shape[1]

    def body(i, carry):
        rest, out = carry
        j = nb - 1 - i
        r_j = lax.dynamic_slice_in_dim(rest, j * BLOCK, BLOCK, 0)
        p_j = lax.dynamic_index_in_dim(prod, j, 0, keepdims=False)
        d_j = lax.dynamic_index_in_dim(inv_diag, j, 0, keepdims=False)
        v_j = jnp.einsum("ji,jk->ik", p_j, r_j, precision=HIGH) * d_j[:, None]
        rows = lax.dynamic_slice_in_dim(tile, j * BLOCK, BLOCK, 0)
        rest = rest - split_dot_t(rows, v_j)
        out = lax.dynamic_update_slice_in_dim(out, v_j, j * BLOCK, 0)
        return rest, out

    _, out = lax.fori_loop(0, nb, body, (rhs, jnp.zeros((n, cols), jnp.float32)))
    return out


def on_device(front, anc_weight, solved, owners, indices, counts, rhs_side):
    row_count = lax.axis_size("row")
    col_count = lax.axis_size("col")
    tiles_block = row_count * col_count
    row_index = lax.axis_index("row")
    col_index = lax.axis_index("col")
    tile_rows = indices.shape[1]
    columns = solved.shape[1]
    self_id = row_index * col_count + col_index
    owner_grid = owners.reshape(row_count, tiles_block)
    mine = (owner_grid == self_id).astype(jnp.int32)
    position = jnp.sum(mine * jnp.arange(tiles_block, dtype=jnp.int32)[None, :], axis=1)
    tile_ids = jnp.arange(row_count, dtype=jnp.int32) * tiles_block + position
    local_rows = indices[tile_ids]
    live_rows = jnp.arange(tile_rows, dtype=jnp.int32)[None, :] < counts[tile_ids][:, None]
    picked = solved[local_rows.reshape(-1)].reshape(row_count, tile_rows, columns)
    picked = jnp.where(live_rows[:, :, None], picked, jnp.zeros_like(picked))
    block_owners = lax.dynamic_slice_in_dim(owners, row_index * tiles_block, tiles_block)
    outgoing = jnp.broadcast_to(picked[:, None], (row_count, col_count, tile_rows, columns))
    outgoing = outgoing.reshape(row_count * col_count * tile_rows, columns)
    received = lax.all_to_all(outgoing, ("row", "col"), split_axis=0, concat_axis=0, tiled=True)
    slot_rows = received.reshape(tiles_block, tile_rows, columns)
    anc_values = slot_rows[block_owners].reshape(tiles_block * tile_rows, columns)
    w_rows = anc_weight.shape[0]
    both = jnp.concatenate([anc_weight, front], axis=0)
    for axis in ("xh", "y", "z"):
        both = lax.all_gather(both, axis, axis=0, tiled=True)
    both = both.reshape(-1, w_rows + front.shape[0], both.shape[1])
    weight_tile = both[:, :w_rows].reshape(-1, both.shape[2])
    front_tile = both[:, w_rows:].reshape(-1, both.shape[2])
    width = front_tile.shape[1]
    anc_total = lax.dot_general(
        weight_tile, anc_values, (((0,), (0,)), ((), ())), preferred_element_type=jnp.float32
    )
    prod, inv_diag = prepare(front_tile)
    rhs_values = rhs_side.astype(jnp.float32)
    down = [(1, 0)]
    left = [(1, 0)]
    right = [(0, 1)]

    own_one = anc_total.astype(jnp.bfloat16)
    other_one = lax.ppermute(own_one, "row", [(0, 1)])
    reduced_one = rhs_values - own_one.astype(jnp.float32) - other_one.astype(jnp.float32)
    sol_one = kernel_solve(front_tile, prod, inv_diag, reduced_one)
    got_one = lax.ppermute(sol_one, "col", left)
    sol_one = jnp.where(col_index == 1, sol_one, got_one)

    own_zero = (anc_total + split_dot_t(front_tile, sol_one.astype(jnp.float32))).astype(jnp.bfloat16)
    own_zero = jnp.where(row_index == 0, anc_total.astype(jnp.bfloat16), own_zero)
    other_zero = lax.ppermute(own_zero, "row", down)
    reduced_zero = rhs_values - own_zero.astype(jnp.float32) - other_zero.astype(jnp.float32)
    sol_zero = kernel_solve(front_tile, prod, inv_diag, reduced_zero)
    got_zero = lax.ppermute(sol_zero, "col", right)
    sol_zero = jnp.where(col_index == 0, sol_zero, got_zero)
    return jnp.where(row_index == 1, sol_one, sol_zero)


def solution(mesh):
    dims = dict(mesh.shape)
    rhs_split = (dims["rhs"] // 8, 4, 2)
    sub = jax.sharding.Mesh(
        mesh.devices.reshape(dims["row"], dims["col"], *rhs_split), ("row", "col", "z", "y", "xh")
    )
    rhs = ("z", "y", "xh")
    placed = (
        P(("row",) + rhs, "col"),
        P(("row",) + rhs, "col"),
        P(("row", "col"), rhs),
        P(),
        P(),
        P(),
        P("row", rhs),
    )
    return jax.shard_map(
        on_device, mesh=sub, in_specs=placed, out_specs=P("row", rhs), check_vma=False
    )
```

```python
import jax
import jax.numpy as jnp
from jax import lax
from jax.sharding import PartitionSpec as P
from jax.experimental import pallas as pl
from jax.experimental.pallas import tpu as pltpu

BLOCK = 128
HIGH = lax.Precision.HIGHEST


def split_dot_t(mat_bf16, vec_f32):
    hi = vec_f32.astype(jnp.bfloat16)
    lo = (vec_f32 - hi.astype(jnp.float32)).astype(jnp.bfloat16)
    dims = (((0,), (0,)), ((), ()))
    out = lax.dot_general(mat_bf16, hi, dims, preferred_element_type=jnp.float32)
    return out + lax.dot_general(mat_bf16, lo, dims, preferred_element_type=jnp.float32)


def split_bf16(x):
    hi = x.astype(jnp.bfloat16)
    return hi, (x - hi.astype(jnp.float32)).astype(jnp.bfloat16)


def mm3(a, b):
    a_hi, a_lo = split_bf16(a)
    b_hi, b_lo = split_bf16(b)
    eq = "bij,bjk->bik"
    out = jnp.einsum(eq, a_hi, b_hi, preferred_element_type=jnp.float32)
    out = out + jnp.einsum(eq, a_lo, b_hi, preferred_element_type=jnp.float32)
    return out + jnp.einsum(eq, a_hi, b_lo, preferred_element_type=jnp.float32)


def prepare(tile):
    n = tile.shape[0]
    nb = n // BLOCK
    starts = jnp.arange(nb, dtype=jnp.int32) * BLOCK
    blocks = jax.vmap(lambda s: lax.dynamic_slice(tile, (s, s), (BLOCK, BLOCK)))(starts)
    blocks = blocks.astype(jnp.float32)
    eye = jnp.eye(BLOCK, dtype=jnp.float32)
    diag = jnp.sum(blocks * eye[None], axis=2)
    lower = jnp.tril(jnp.ones((BLOCK, BLOCK), jnp.bool_), -1)
    nil = jnp.where(lower[None], blocks / diag[:, :, None], 0.0)
    prod = eye[None] - nil
    power = nil
    steps = 1
    while 2 ** steps < BLOCK:
        power = mm3(power, power)
        prod = mm3(prod, eye[None] + power)
        steps += 1
    return prod, 1.0 / diag


def solve_kernel(f_ref, p_ref, d_ref, r_ref, o_ref, rest_ref):
    nb = p_ref.shape[0]
    rest_ref[...] = r_ref[...]

    def body(i, carry):
        j = nb - 1 - i
        start = pl.multiple_of(j * BLOCK, BLOCK)
        r_hi, r_lo = split_bf16(rest_ref[:, pl.ds(start, BLOCK)])
        p_hi, p_lo = split_bf16(p_ref[j])
        v = jnp.dot(r_hi, p_hi, preferred_element_type=jnp.float32)
        v = v + jnp.dot(r_lo, p_hi, preferred_element_type=jnp.float32)
        v = v + jnp.dot(r_hi, p_lo, preferred_element_type=jnp.float32)
        v = v * d_ref[pl.ds(j, 1), :]
        v_hi, v_lo = split_bf16(v)
        rows = f_ref[pl.ds(start, BLOCK), :]
        upd = jnp.dot(v_hi, rows, preferred_element_type=jnp.float32)
        upd = upd + jnp.dot(v_lo, rows, preferred_element_type=jnp.float32)
        rest_ref[...] = rest_ref[...] - upd
        o_ref[:, pl.ds(start, BLOCK)] = v.astype(o_ref.dtype)
        return carry

    lax.fori_loop(0, nb, body, 0)


def kernel_solve(tile, prod, inv_diag, rhs):
    n = tile.shape[0]
    cols = rhs.shape[1]
    vmem = pl.BlockSpec(memory_space=pltpu.VMEM)
    out_t = pl.pallas_call(
        solve_kernel,
        out_shape=jax.ShapeDtypeStruct((cols, n), jnp.bfloat16),
        in_specs=[vmem, vmem, vmem, vmem],
        out_specs=vmem,
        scratch_shapes=[pltpu.VMEM((cols, n), jnp.float32)],
        compiler_params=pltpu.CompilerParams(vmem_limit_bytes=48 * 1024 * 1024),
    )(tile, prod, inv_diag, rhs.T)
    return out_t.T


def apply_solve(tile, prod, inv_diag, rhs):
    n = tile.shape[0]
    nb = n // BLOCK
    cols = rhs.shape[1]

    def body(i, carry):
        rest, out = carry
        j = nb - 1 - i
        r_j = lax.dynamic_slice_in_dim(rest, j * BLOCK, BLOCK, 0)
        p_j = lax.dynamic_index_in_dim(prod, j, 0, keepdims=False)
        d_j = lax.dynamic_index_in_dim(inv_diag, j, 0, keepdims=False)
        v_j = jnp.einsum("ji,jk->ik", p_j, r_j, precision=HIGH) * d_j[:, None]
        rows = lax.dynamic_slice_in_dim(tile, j * BLOCK, BLOCK, 0)
        rest = rest - split_dot_t(rows, v_j)
        out = lax.dynamic_update_slice_in_dim(out, v_j, j * BLOCK, 0)
        return rest, out

    _, out = lax.fori_loop(0, nb, body, (rhs, jnp.zeros((n, cols), jnp.float32)))
    return out


def on_device(front, anc_weight, solved, owners, indices, counts, rhs_side):
    row_count = lax.axis_size("row")
    col_count = lax.axis_size("col")
    tiles_block = row_count * col_count
    row_index = lax.axis_index("row")
    col_index = lax.axis_index("col")
    tile_rows = indices.shape[1]
    columns = solved.shape[1]
    self_id = row_index * col_count + col_index
    owner_grid = owners.reshape(row_count, tiles_block)
    mine = (owner_grid == self_id).astype(jnp.int32)
    position = jnp.sum(mine * jnp.arange(tiles_block, dtype=jnp.int32)[None, :], axis=1)
    tile_ids = jnp.arange(row_count, dtype=jnp.int32) * tiles_block + position
    local_rows = indices[tile_ids]
    live_rows = jnp.arange(tile_rows, dtype=jnp.int32)[None, :] < counts[tile_ids][:, None]
    picked = solved[local_rows.reshape(-1)].reshape(row_count, tile_rows, columns)
    picked = jnp.where(live_rows[:, :, None], picked, jnp.zeros_like(picked))
    block_owners = lax.dynamic_slice_in_dim(owners, row_index * tiles_block, tiles_block)
    outgoing = jnp.broadcast_to(picked[:, None], (row_count, col_count, tile_rows, columns))
    outgoing = outgoing.reshape(row_count * col_count * tile_rows, columns)
    received = lax.all_to_all(outgoing, ("row", "col"), split_axis=0, concat_axis=0, tiled=True)
    slot_rows = received.reshape(tiles_block, tile_rows, columns)
    anc_values = slot_rows[block_owners].reshape(tiles_block * tile_rows, columns)
    w_rows = anc_weight.shape[0]
    both = jnp.concatenate([anc_weight, front], axis=0)
    for axis in ("xh", "y", "z"):
        both = lax.all_gather(both, axis, axis=0, tiled=True)
    both = both.reshape(-1, w_rows + front.shape[0], both.shape[1])
    weight_tile = both[:, :w_rows].reshape(-1, both.shape[2])
    front_tile = both[:, w_rows:].reshape(-1, both.shape[2])
    width = front_tile.shape[1]
    anc_total = lax.dot_general(
        weight_tile, anc_values, (((0,), (0,)), ((), ())), preferred_element_type=jnp.float32
    )
    prod, inv_diag = prepare(front_tile)
    rhs_values = rhs_side.astype(jnp.float32)
    down = [(1, 0)]
    left = [(1, 0)]
    right = [(0, 1)]

    own_one = anc_total.astype(jnp.bfloat16)
    other_one = lax.ppermute(own_one, "row", [(0, 1)])
    reduced_one = rhs_values - own_one.astype(jnp.float32) - other_one.astype(jnp.float32)
    sol_one = kernel_solve(front_tile, prod, inv_diag, reduced_one)
    got_one = lax.ppermute(sol_one, "col", left)
    sol_one = jnp.where(col_index == 1, sol_one, got_one)

    own_zero = (anc_total + split_dot_t(front_tile, sol_one.astype(jnp.float32))).astype(jnp.bfloat16)
    own_zero = jnp.where(row_index == 0, anc_total.astype(jnp.bfloat16), own_zero)
    other_zero = lax.ppermute(own_zero, "row", down)
    reduced_zero = rhs_values - own_zero.astype(jnp.float32) - other_zero.astype(jnp.float32)
    sol_zero = kernel_solve(front_tile, prod, inv_diag, reduced_zero)
    got_zero = lax.ppermute(sol_zero, "col", right)
    sol_zero = jnp.where(col_index == 0, sol_zero, got_zero)
    return jnp.where(row_index == 1, sol_one, sol_zero)


def solution(mesh):
    dims = dict(mesh.shape)
    rhs_split = (dims["rhs"] // 8, 4, 2)
    sub = jax.sharding.Mesh(
        mesh.devices.reshape(dims["row"], dims["col"], *rhs_split), ("row", "col", "z", "y", "xh")
    )
    rhs = ("z", "y", "xh")
    placed = (
        P(("row",) + rhs, "col"),
        P(("row",) + rhs, "col"),
        P(("row", "col"), rhs),
        P(),
        P(),
        P(),
        P("row", rhs),
    )
    return jax.shard_map(
        on_device, mesh=sub, in_specs=placed, out_specs=P("row", rhs), check_vma=False
    )
```

```python
import jax
import jax.numpy as jnp
from jax import lax
from jax.sharding import PartitionSpec as P
from jax.experimental import pallas as pl
from jax.experimental.pallas import tpu as pltpu

BLOCK = 128
HIGH = lax.Precision.HIGHEST


def split_dot_t(mat_bf16, vec_f32):
    hi = vec_f32.astype(jnp.bfloat16)
    lo = (vec_f32 - hi.astype(jnp.float32)).astype(jnp.bfloat16)
    dims = (((0,), (0,)), ((), ()))
    out = lax.dot_general(mat_bf16, hi, dims, preferred_element_type=jnp.float32)
    return out + lax.dot_general(mat_bf16, lo, dims, preferred_element_type=jnp.float32)


def split_bf16(x):
    hi = x.astype(jnp.bfloat16)
    return hi, (x - hi.astype(jnp.float32)).astype(jnp.bfloat16)


def mm3(a, b):
    a_hi, a_lo = split_bf16(a)
    b_hi, b_lo = split_bf16(b)
    eq = "bij,bjk->bik"
    out = jnp.einsum(eq, a_hi, b_hi, preferred_element_type=jnp.float32)
    out = out + jnp.einsum(eq, a_lo, b_hi, preferred_element_type=jnp.float32)
    return out + jnp.einsum(eq, a_hi, b_lo, preferred_element_type=jnp.float32)


def copy_kernel(t_ref, o_ref):
    o_ref[0] = t_ref[...]


def prepare(tile):
    n = tile.shape[0]
    nb = n // BLOCK
    blocks = pl.pallas_call(
        copy_kernel,
        grid=(nb,),
        in_specs=[pl.BlockSpec((BLOCK, BLOCK), lambda j: (j, j))],
        out_specs=pl.BlockSpec((1, BLOCK, BLOCK), lambda j: (j, 0, 0)),
        out_shape=jax.ShapeDtypeStruct((nb, BLOCK, BLOCK), tile.dtype),
    )(tile).astype(jnp.float32)
    eye = jnp.eye(BLOCK, dtype=jnp.float32)
    diag = jnp.sum(blocks * eye[None], axis=2)
    lower = jnp.tril(jnp.ones((BLOCK, BLOCK), jnp.bool_), -1)
    nil = jnp.where(lower[None], blocks / diag[:, :, None], 0.0)
    prod = eye[None] - nil
    power = nil
    steps = 1
    while 2 ** steps < BLOCK:
        power = mm3(power, power)
        prod = mm3(prod, eye[None] + power)
        steps += 1
    return prod, 1.0 / diag


def solve_kernel(f_ref, p_ref, d_ref, r_ref, o_ref, rest_ref):
    nb = p_ref.shape[0]
    rest_ref[...] = r_ref[...]

    def body(i, carry):
        j = nb - 1 - i
        start = pl.multiple_of(j * BLOCK, BLOCK)
        r_hi, r_lo = split_bf16(rest_ref[:, pl.ds(start, BLOCK)])
        p_hi, p_lo = split_bf16(p_ref[j])
        v = jnp.dot(r_hi, p_hi, preferred_element_type=jnp.float32)
        v = v + jnp.dot(r_lo, p_hi, preferred_element_type=jnp.float32)
        v = v + jnp.dot(r_hi, p_lo, preferred_element_type=jnp.float32)
        v = v * d_ref[pl.ds(j, 1), :]
        v_hi, v_lo = split_bf16(v)
        rows = f_ref[pl.ds(start, BLOCK), : rest_ref.shape[1]]
        upd = jnp.dot(v_hi, rows, preferred_element_type=jnp.float32)
        upd = upd + jnp.dot(v_lo, rows, preferred_element_type=jnp.float32)
        rest_ref[...] = rest_ref[...] - upd
        o_ref[:, pl.ds(start, BLOCK)] = v.astype(o_ref.dtype)
        return carry

    lax.fori_loop(0, nb, body, 0)


def kernel_solve(tile, prod, inv_diag, rhs):
    n = rhs.shape[0]
    cols = rhs.shape[1]
    vmem = pl.BlockSpec(memory_space=pltpu.VMEM)
    out_t = pl.pallas_call(
        solve_kernel,
        out_shape=jax.ShapeDtypeStruct((cols, n), jnp.bfloat16),
        in_specs=[vmem, vmem, vmem, vmem],
        out_specs=vmem,
        scratch_shapes=[pltpu.VMEM((cols, n), jnp.float32)],
        compiler_params=pltpu.CompilerParams(vmem_limit_bytes=48 * 1024 * 1024),
    )(tile, prod, inv_diag, rhs.T)
    return out_t.T


def apply_solve(tile, prod, inv_diag, rhs):
    n = tile.shape[0]
    nb = n // BLOCK
    cols = rhs.shape[1]

    def body(i, carry):
        rest, out = carry
        j = nb - 1 - i
        r_j = lax.dynamic_slice_in_dim(rest, j * BLOCK, BLOCK, 0)
        p_j = lax.dynamic_index_in_dim(prod, j, 0, keepdims=False)
        d_j = lax.dynamic_index_in_dim(inv_diag, j, 0, keepdims=False)
        v_j = jnp.einsum("ji,jk->ik", p_j, r_j, precision=HIGH) * d_j[:, None]
        rows = lax.dynamic_slice_in_dim(tile, j * BLOCK, BLOCK, 0)
        rest = rest - split_dot_t(rows, v_j)
        out = lax.dynamic_update_slice_in_dim(out, v_j, j * BLOCK, 0)
        return rest, out

    _, out = lax.fori_loop(0, nb, body, (rhs, jnp.zeros((n, cols), jnp.float32)))
    return out


def on_device(front, anc_weight, solved, owners, indices, counts, rhs_side):
    row_count = lax.axis_size("row")
    col_count = lax.axis_size("col")
    tiles_block = row_count * col_count
    row_index = lax.axis_index("row")
    col_index = lax.axis_index("col")
    tile_rows = indices.shape[1]
    columns = solved.shape[1]
    self_id = row_index * col_count + col_index
    owner_grid = owners.reshape(row_count, tiles_block)
    mine = (owner_grid == self_id).astype(jnp.int32)
    position = jnp.sum(mine * jnp.arange(tiles_block, dtype=jnp.int32)[None, :], axis=1)
    tile_ids = jnp.arange(row_count, dtype=jnp.int32) * tiles_block + position
    local_rows = indices[tile_ids]
    live_rows = jnp.arange(tile_rows, dtype=jnp.int32)[None, :] < counts[tile_ids][:, None]
    picked = solved[local_rows.reshape(-1)].reshape(row_count, tile_rows, columns)
    picked = jnp.where(live_rows[:, :, None], picked, jnp.zeros_like(picked))
    block_owners = lax.dynamic_slice_in_dim(owners, row_index * tiles_block, tiles_block)
    outgoing = jnp.broadcast_to(picked[:, None], (row_count, col_count, tile_rows, columns))
    outgoing = outgoing.reshape(row_count * col_count * tile_rows, columns)
    received = lax.all_to_all(outgoing, ("row", "col"), split_axis=0, concat_axis=0, tiled=True)
    slot_rows = received.reshape(tiles_block, tile_rows, columns)
    anc_values = slot_rows[block_owners].reshape(tiles_block * tile_rows, columns)
    shard_rows, width = front.shape
    w_rows = anc_weight.shape[0]
    fold = shard_rows // w_rows
    both = jnp.concatenate([front, anc_weight.reshape(shard_rows, width // fold)], axis=1)
    for axis in ("xh", "y", "z"):
        both = lax.all_gather(both, axis, axis=0, tiled=True)
    front_tile = both
    weight_tile = both[:, width:].reshape(-1, w_rows, fold, width // fold).reshape(-1, width)
    anc_total = lax.dot_general(
        weight_tile, anc_values, (((0,), (0,)), ((), ())), preferred_element_type=jnp.float32
    )
    prod, inv_diag = prepare(front_tile)
    rhs_values = rhs_side.astype(jnp.float32)
    down = [(1, 0)]
    left = [(1, 0)]
    right = [(0, 1)]

    own_one = anc_total.astype(jnp.bfloat16)
    other_one = lax.ppermute(own_one, "row", [(0, 1)])
    reduced_one = rhs_values - own_one.astype(jnp.float32) - other_one.astype(jnp.float32)
    sol_one = kernel_solve(front_tile, prod, inv_diag, reduced_one)
    got_one = lax.ppermute(sol_one, "col", left)
    sol_one = jnp.where(col_index == 1, sol_one, got_one)

    own_zero = (anc_total + split_dot_t(front_tile[:, :width], sol_one.astype(jnp.float32))).astype(jnp.bfloat16)
    own_zero = jnp.where(row_index == 0, anc_total.astype(jnp.bfloat16), own_zero)
    other_zero = lax.ppermute(own_zero, "row", down)
    reduced_zero = rhs_values - own_zero.astype(jnp.float32) - other_zero.astype(jnp.float32)
    sol_zero = kernel_solve(front_tile, prod, inv_diag, reduced_zero)
    got_zero = lax.ppermute(sol_zero, "col", right)
    sol_zero = jnp.where(col_index == 0, sol_zero, got_zero)
    return jnp.where(row_index == 1, sol_one, sol_zero)


def solution(mesh):
    dims = dict(mesh.shape)
    rhs_split = (dims["rhs"] // 8, 4, 2)
    sub = jax.sharding.Mesh(
        mesh.devices.reshape(dims["row"], dims["col"], *rhs_split), ("row", "col", "z", "y", "xh")
    )
    rhs = ("z", "y", "xh")
    placed = (
        P(("row",) + rhs, "col"),
        P(("row",) + rhs, "col"),
        P(("row", "col"), rhs),
        P(),
        P(),
        P(),
        P("row", rhs),
    )
    return jax.shard_map(
        on_device, mesh=sub, in_specs=placed, out_specs=P("row", rhs), check_vma=False
    )
```

```python
import jax
import jax.numpy as jnp
from jax import lax
from jax.sharding import PartitionSpec as P
from jax.experimental import pallas as pl
from jax.experimental.pallas import tpu as pltpu

BLOCK = 128
HIGH = lax.Precision.HIGHEST


def split_dot_t(mat_bf16, vec_f32):
    hi = vec_f32.astype(jnp.bfloat16)
    lo = (vec_f32 - hi.astype(jnp.float32)).astype(jnp.bfloat16)
    dims = (((0,), (0,)), ((), ()))
    out = lax.dot_general(mat_bf16, hi, dims, preferred_element_type=jnp.float32)
    return out + lax.dot_general(mat_bf16, lo, dims, preferred_element_type=jnp.float32)


def split_bf16(x):
    hi = x.astype(jnp.bfloat16)
    return hi, (x - hi.astype(jnp.float32)).astype(jnp.bfloat16)


def mm3(a, b):
    a_hi, a_lo = split_bf16(a)
    b_hi, b_lo = split_bf16(b)
    eq = "bij,bjk->bik"
    out = jnp.einsum(eq, a_hi, b_hi, preferred_element_type=jnp.float32)
    out = out + jnp.einsum(eq, a_lo, b_hi, preferred_element_type=jnp.float32)
    return out + jnp.einsum(eq, a_hi, b_lo, preferred_element_type=jnp.float32)


def diag_kernel(t_hbm, o_ref, sems):
    nb = o_ref.shape[0]
    copies = [
        pltpu.make_async_copy(
            t_hbm.at[pl.ds(j * BLOCK, BLOCK), pl.ds(j * BLOCK, BLOCK)], o_ref.at[j], sems.at[j]
        )
        for j in range(nb)
    ]
    for one in copies:
        one.start()
    for one in copies:
        one.wait()


def prepare(tile):
    n = tile.shape[0]
    nb = n // BLOCK
    blocks = pl.pallas_call(
        diag_kernel,
        in_specs=[pl.BlockSpec(memory_space=pl.ANY)],
        out_specs=pl.BlockSpec(memory_space=pltpu.VMEM),
        out_shape=jax.ShapeDtypeStruct((nb, BLOCK, BLOCK), tile.dtype),
        scratch_shapes=[pltpu.SemaphoreType.DMA((nb,))],
    )(tile).astype(jnp.float32)
    eye = jnp.eye(BLOCK, dtype=jnp.float32)
    diag = jnp.sum(blocks * eye[None], axis=2)
    lower = jnp.tril(jnp.ones((BLOCK, BLOCK), jnp.bool_), -1)
    nil = jnp.where(lower[None], blocks / diag[:, :, None], 0.0)
    prod = eye[None] - nil
    power = nil
    steps = 1
    while 2 ** steps < BLOCK:
        power = mm3(power, power)
        prod = mm3(prod, eye[None] + power)
        steps += 1
    return prod, 1.0 / diag


def solve_kernel(f_ref, p_ref, d_ref, r_ref, o_ref, rest_ref):
    nb = p_ref.shape[0]
    rest_ref[...] = r_ref[...]

    def body(i, carry):
        j = nb - 1 - i
        start = pl.multiple_of(j * BLOCK, BLOCK)
        r_hi, r_lo = split_bf16(rest_ref[:, pl.ds(start, BLOCK)])
        p_hi, p_lo = split_bf16(p_ref[j])
        v = jnp.dot(r_hi, p_hi, preferred_element_type=jnp.float32)
        v = v + jnp.dot(r_lo, p_hi, preferred_element_type=jnp.float32)
        v = v + jnp.dot(r_hi, p_lo, preferred_element_type=jnp.float32)
        v = v * d_ref[pl.ds(j, 1), :]
        v_hi, v_lo = split_bf16(v)
        rows = f_ref[pl.ds(start, BLOCK), : rest_ref.shape[1]]
        upd = jnp.dot(v_hi, rows, preferred_element_type=jnp.float32)
        upd = upd + jnp.dot(v_lo, rows, preferred_element_type=jnp.float32)
        rest_ref[...] = rest_ref[...] - upd
        o_ref[:, pl.ds(start, BLOCK)] = v.astype(o_ref.dtype)
        return carry

    lax.fori_loop(0, nb, body, 0)


def kernel_solve(tile, prod, inv_diag, rhs):
    n = rhs.shape[0]
    cols = rhs.shape[1]
    vmem = pl.BlockSpec(memory_space=pltpu.VMEM)
    out_t = pl.pallas_call(
        solve_kernel,
        out_shape=jax.ShapeDtypeStruct((cols, n), jnp.bfloat16),
        in_specs=[vmem, vmem, vmem, vmem],
        out_specs=vmem,
        scratch_shapes=[pltpu.VMEM((cols, n), jnp.float32)],
        compiler_params=pltpu.CompilerParams(vmem_limit_bytes=48 * 1024 * 1024),
    )(tile, prod, inv_diag, rhs.T)
    return out_t.T


def apply_solve(tile, prod, inv_diag, rhs):
    n = tile.shape[0]
    nb = n // BLOCK
    cols = rhs.shape[1]

    def body(i, carry):
        rest, out = carry
        j = nb - 1 - i
        r_j = lax.dynamic_slice_in_dim(rest, j * BLOCK, BLOCK, 0)
        p_j = lax.dynamic_index_in_dim(prod, j, 0, keepdims=False)
        d_j = lax.dynamic_index_in_dim(inv_diag, j, 0, keepdims=False)
        v_j = jnp.einsum("ji,jk->ik", p_j, r_j, precision=HIGH) * d_j[:, None]
        rows = lax.dynamic_slice_in_dim(tile, j * BLOCK, BLOCK, 0)
        rest = rest - split_dot_t(rows, v_j)
        out = lax.dynamic_update_slice_in_dim(out, v_j, j * BLOCK, 0)
        return rest, out

    _, out = lax.fori_loop(0, nb, body, (rhs, jnp.zeros((n, cols), jnp.float32)))
    return out


def on_device(front, anc_weight, solved, owners, indices, counts, rhs_side):
    row_count = lax.axis_size("row")
    col_count = lax.axis_size("col")
    tiles_block = row_count * col_count
    row_index = lax.axis_index("row")
    col_index = lax.axis_index("col")
    tile_rows = indices.shape[1]
    columns = solved.shape[1]
    self_id = row_index * col_count + col_index
    owner_grid = owners.reshape(row_count, tiles_block)
    mine = (owner_grid == self_id).astype(jnp.int32)
    position = jnp.sum(mine * jnp.arange(tiles_block, dtype=jnp.int32)[None, :], axis=1)
    tile_ids = jnp.arange(row_count, dtype=jnp.int32) * tiles_block + position
    local_rows = indices[tile_ids]
    live_rows = jnp.arange(tile_rows, dtype=jnp.int32)[None, :] < counts[tile_ids][:, None]
    picked = solved[local_rows.reshape(-1)].reshape(row_count, tile_rows, columns)
    picked = jnp.where(live_rows[:, :, None], picked, jnp.zeros_like(picked))
    block_owners = lax.dynamic_slice_in_dim(owners, row_index * tiles_block, tiles_block)
    outgoing = jnp.broadcast_to(picked[:, None], (row_count, col_count, tile_rows, columns))
    outgoing = outgoing.reshape(row_count * col_count * tile_rows, columns)
    received = lax.all_to_all(outgoing, ("row", "col"), split_axis=0, concat_axis=0, tiled=True)
    slot_rows = received.reshape(tiles_block, tile_rows, columns)
    anc_values = slot_rows[block_owners].reshape(tiles_block * tile_rows, columns)
    shard_rows, width = front.shape
    w_rows = anc_weight.shape[0]
    fold = shard_rows // w_rows
    both = jnp.concatenate([front, anc_weight.reshape(shard_rows, width // fold)], axis=1)
    for axis in ("xh", "z", "y"):
        both = lax.all_gather(both, axis, axis=0, tiled=True)
    n_y, n_z = lax.axis_size("y"), lax.axis_size("z")
    both = both.reshape(n_y, n_z, -1, both.shape[1]).transpose(1, 0, 2, 3).reshape(-1, both.shape[1])
    front_tile = both
    weight_tile = both[:, width:].reshape(-1, w_rows, fold, width // fold).reshape(-1, width)
    anc_total = lax.dot_general(
        weight_tile, anc_values, (((0,), (0,)), ((), ())), preferred_element_type=jnp.float32
    )
    prod, inv_diag = prepare(front_tile)
    rhs_values = rhs_side.astype(jnp.float32)
    down = [(1, 0)]
    left = [(1, 0)]
    right = [(0, 1)]

    own_one = anc_total.astype(jnp.bfloat16)
    other_one = lax.ppermute(own_one, "row", [(0, 1)])
    reduced_one = rhs_values - own_one.astype(jnp.float32) - other_one.astype(jnp.float32)
    sol_one = kernel_solve(front_tile, prod, inv_diag, reduced_one)
    got_one = lax.ppermute(sol_one, "col", left)
    sol_one = jnp.where(col_index == 1, sol_one, got_one)

    front_term = lax.dot_general(
        front_tile[:, :width], sol_one, (((0,), (0,)), ((), ())), preferred_element_type=jnp.float32
    )
    own_zero = (anc_total + front_term).astype(jnp.bfloat16)
    own_zero = jnp.where(row_index == 0, anc_total.astype(jnp.bfloat16), own_zero)
    other_zero = lax.ppermute(own_zero, "row", down)
    reduced_zero = rhs_values - own_zero.astype(jnp.float32) - other_zero.astype(jnp.float32)
    sol_zero = kernel_solve(front_tile, prod, inv_diag, reduced_zero)
    got_zero = lax.ppermute(sol_zero, "col", right)
    sol_zero = jnp.where(col_index == 0, sol_zero, got_zero)
    return jnp.where(row_index == 1, sol_one, sol_zero)


def solution(mesh):
    dims = dict(mesh.shape)
    rhs_split = (dims["rhs"] // 8, 4, 2)
    sub = jax.sharding.Mesh(
        mesh.devices.reshape(dims["row"], dims["col"], *rhs_split), ("row", "col", "z", "y", "xh")
    )
    rhs = ("z", "y", "xh")
    placed = (
        P(("row",) + rhs, "col"),
        P(("row",) + rhs, "col"),
        P(("row", "col"), rhs),
        P(),
        P(),
        P(),
        P("row", rhs),
    )
    return jax.shard_map(
        on_device, mesh=sub, in_specs=placed, out_specs=P("row", rhs), check_vma=False
    )
```

```python
import jax
import jax.numpy as jnp
from jax import lax
from jax.sharding import PartitionSpec as P
from jax.experimental import pallas as pl
from jax.experimental.pallas import tpu as pltpu

BLOCK = 128
HIGH = lax.Precision.HIGHEST


def split_dot_t(mat_bf16, vec_f32):
    hi = vec_f32.astype(jnp.bfloat16)
    lo = (vec_f32 - hi.astype(jnp.float32)).astype(jnp.bfloat16)
    dims = (((0,), (0,)), ((), ()))
    out = lax.dot_general(mat_bf16, hi, dims, preferred_element_type=jnp.float32)
    return out + lax.dot_general(mat_bf16, lo, dims, preferred_element_type=jnp.float32)


def split_bf16(x):
    hi = x.astype(jnp.bfloat16)
    return hi, (x - hi.astype(jnp.float32)).astype(jnp.bfloat16)


def mm3(a, b):
    a_hi, a_lo = split_bf16(a)
    b_hi, b_lo = split_bf16(b)
    eq = "bij,bjk->bik"
    out = jnp.einsum(eq, a_hi, b_hi, preferred_element_type=jnp.float32)
    out = out + jnp.einsum(eq, a_lo, b_hi, preferred_element_type=jnp.float32)
    return out + jnp.einsum(eq, a_hi, b_lo, preferred_element_type=jnp.float32)


def diag_kernel(t_hbm, o_ref, sems):
    nb = o_ref.shape[0]
    copies = [
        pltpu.make_async_copy(
            t_hbm.at[pl.ds(j * BLOCK, BLOCK), pl.ds(j * BLOCK, BLOCK)], o_ref.at[j], sems.at[j]
        )
        for j in range(nb)
    ]
    for one in copies:
        one.start()
    for one in copies:
        one.wait()


def prepare(tile):
    n = tile.shape[0]
    nb = n // BLOCK
    blocks = pl.pallas_call(
        diag_kernel,
        in_specs=[pl.BlockSpec(memory_space=pl.ANY)],
        out_specs=pl.BlockSpec(memory_space=pltpu.VMEM),
        out_shape=jax.ShapeDtypeStruct((nb, BLOCK, BLOCK), tile.dtype),
        scratch_shapes=[pltpu.SemaphoreType.DMA((nb,))],
    )(tile).astype(jnp.float32)
    eye = jnp.eye(BLOCK, dtype=jnp.float32)
    diag = jnp.sum(blocks * eye[None], axis=2)
    lower = jnp.tril(jnp.ones((BLOCK, BLOCK), jnp.bool_), -1)
    nil = jnp.where(lower[None], blocks / diag[:, :, None], 0.0)
    prod = eye[None] - nil
    power = nil
    steps = 1
    while 2 ** steps < BLOCK:
        power = mm3(power, power)
        prod = mm3(prod, eye[None] + power)
        steps += 1
    return prod, 1.0 / diag


def solve_kernel(f_ref, p_ref, d_ref, r_ref, o_ref, rest_ref):
    nb = p_ref.shape[0]
    rest_ref[...] = r_ref[...]

    def body(i, carry):
        j = nb - 1 - i
        start = pl.multiple_of(j * BLOCK, BLOCK)
        r_hi, r_lo = split_bf16(rest_ref[:, pl.ds(start, BLOCK)])
        p_hi, p_lo = split_bf16(p_ref[j])
        v = jnp.dot(r_hi, p_hi, preferred_element_type=jnp.float32)
        v = v + jnp.dot(r_lo, p_hi, preferred_element_type=jnp.float32)
        v = v + jnp.dot(r_hi, p_lo, preferred_element_type=jnp.float32)
        v = v * d_ref[pl.ds(j, 1), :]
        v_hi, v_lo = split_bf16(v)
        rows = f_ref[pl.ds(start, BLOCK), : rest_ref.shape[1]]
        upd = jnp.dot(v_hi, rows, preferred_element_type=jnp.float32)
        upd = upd + jnp.dot(v_lo, rows, preferred_element_type=jnp.float32)
        rest_ref[...] = rest_ref[...] - upd
        o_ref[:, pl.ds(start, BLOCK)] = v.astype(o_ref.dtype)
        return carry

    lax.fori_loop(0, nb, body, 0)


def kernel_solve(tile, prod, inv_diag, rhs):
    n = rhs.shape[0]
    cols = rhs.shape[1]
    vmem = pl.BlockSpec(memory_space=pltpu.VMEM)
    out_t = pl.pallas_call(
        solve_kernel,
        out_shape=jax.ShapeDtypeStruct((cols, n), jnp.bfloat16),
        in_specs=[vmem, vmem, vmem, vmem],
        out_specs=vmem,
        scratch_shapes=[pltpu.VMEM((cols, n), jnp.float32)],
        compiler_params=pltpu.CompilerParams(vmem_limit_bytes=48 * 1024 * 1024),
    )(tile, prod, inv_diag, rhs.T)
    return out_t.T


def apply_solve(tile, prod, inv_diag, rhs):
    n = tile.shape[0]
    nb = n // BLOCK
    cols = rhs.shape[1]

    def body(i, carry):
        rest, out = carry
        j = nb - 1 - i
        r_j = lax.dynamic_slice_in_dim(rest, j * BLOCK, BLOCK, 0)
        p_j = lax.dynamic_index_in_dim(prod, j, 0, keepdims=False)
        d_j = lax.dynamic_index_in_dim(inv_diag, j, 0, keepdims=False)
        v_j = jnp.einsum("ji,jk->ik", p_j, r_j, precision=HIGH) * d_j[:, None]
        rows = lax.dynamic_slice_in_dim(tile, j * BLOCK, BLOCK, 0)
        rest = rest - split_dot_t(rows, v_j)
        out = lax.dynamic_update_slice_in_dim(out, v_j, j * BLOCK, 0)
        return rest, out

    _, out = lax.fori_loop(0, nb, body, (rhs, jnp.zeros((n, cols), jnp.float32)))
    return out


def chunked_permute(x, axis, perm, parts=4):
    pieces = jnp.split(x, parts, axis=0)
    return jnp.concatenate([lax.ppermute(p, axis, perm) for p in pieces], axis=0)


def on_device(front, anc_weight, solved, owners, indices, counts, rhs_side):
    row_count = lax.axis_size("row")
    col_count = lax.axis_size("col")
    tiles_block = row_count * col_count
    row_index = lax.axis_index("row")
    col_index = lax.axis_index("col")
    tile_rows = indices.shape[1]
    columns = solved.shape[1]
    self_id = row_index * col_count + col_index
    owner_grid = owners.reshape(row_count, tiles_block)
    mine = (owner_grid == self_id).astype(jnp.int32)
    position = jnp.sum(mine * jnp.arange(tiles_block, dtype=jnp.int32)[None, :], axis=1)
    tile_ids = jnp.arange(row_count, dtype=jnp.int32) * tiles_block + position
    local_rows = indices[tile_ids]
    live_rows = jnp.arange(tile_rows, dtype=jnp.int32)[None, :] < counts[tile_ids][:, None]
    picked = solved[local_rows.reshape(-1)].reshape(row_count, tile_rows, columns)
    picked = jnp.where(live_rows[:, :, None], picked, jnp.zeros_like(picked))
    block_owners = lax.dynamic_slice_in_dim(owners, row_index * tiles_block, tiles_block)
    outgoing = jnp.broadcast_to(picked[:, None], (row_count, col_count, tile_rows, columns))
    outgoing = outgoing.reshape(row_count * col_count * tile_rows, columns)
    received = lax.all_to_all(outgoing, ("row", "col"), split_axis=0, concat_axis=0, tiled=True)
    slot_rows = received.reshape(tiles_block, tile_rows, columns)
    anc_values = slot_rows[block_owners].reshape(tiles_block * tile_rows, columns)
    shard_rows, width = front.shape
    w_rows = anc_weight.shape[0]
    fold = shard_rows // w_rows
    both = jnp.concatenate([front, anc_weight.reshape(shard_rows, width // fold)], axis=1)
    for axis in ("xh", "y", "z"):
        both = lax.all_gather(both, axis, axis=0, tiled=True)
    front_tile = both
    weight_tile = both[:, width:].reshape(-1, w_rows, fold, width // fold).reshape(-1, width)
    anc_total = lax.dot_general(
        weight_tile, anc_values, (((0,), (0,)), ((), ())), preferred_element_type=jnp.float32
    )
    prod, inv_diag = prepare(front_tile)
    rhs_values = rhs_side.astype(jnp.float32)
    down = [(1, 0)]
    left = [(1, 0)]
    right = [(0, 1)]

    own_one = anc_total.astype(jnp.bfloat16)
    other_one = lax.ppermute(own_one, "row", [(0, 1)])
    reduced_one = rhs_values - own_one.astype(jnp.float32) - other_one.astype(jnp.float32)
    sol_one = kernel_solve(front_tile, prod, inv_diag, reduced_one)
    got_one = chunked_permute(sol_one, "col", left)
    sol_one = jnp.where(col_index == 1, sol_one, got_one)

    front_term = lax.dot_general(
        front_tile[:, :width], sol_one, (((0,), (0,)), ((), ())), preferred_element_type=jnp.float32
    )
    own_zero = (anc_total + front_term).astype(jnp.bfloat16)
    own_zero = jnp.where(row_index == 0, anc_total.astype(jnp.bfloat16), own_zero)
    other_zero = lax.ppermute(own_zero, "row", down)
    reduced_zero = rhs_values - own_zero.astype(jnp.float32) - other_zero.astype(jnp.float32)
    sol_zero = kernel_solve(front_tile, prod, inv_diag, reduced_zero)
    got_zero = chunked_permute(sol_zero, "col", right)
    sol_zero = jnp.where(col_index == 0, sol_zero, got_zero)
    return jnp.where(row_index == 1, sol_one, sol_zero)


def solution(mesh):
    dims = dict(mesh.shape)
    rhs_split = (dims["rhs"] // 8, 4, 2)
    sub = jax.sharding.Mesh(
        mesh.devices.reshape(dims["row"], dims["col"], *rhs_split), ("row", "col", "z", "y", "xh")
    )
    rhs = ("z", "y", "xh")
    placed = (
        P(("row",) + rhs, "col"),
        P(("row",) + rhs, "col"),
        P(("row", "col"), rhs),
        P(),
        P(),
        P(),
        P("row", rhs),
    )
    return jax.shard_map(
        on_device, mesh=sub, in_specs=placed, out_specs=P("row", rhs), check_vma=False
    )
```

```python
import jax
import jax.numpy as jnp
from jax import lax
from jax.sharding import PartitionSpec as P
from jax.experimental import pallas as pl
from jax.experimental.pallas import tpu as pltpu

BLOCK = 128


def split_bf16(x):
    hi = x.astype(jnp.bfloat16)
    return hi, (x - hi.astype(jnp.float32)).astype(jnp.bfloat16)


def mm3(a, b):
    a_hi, a_lo = split_bf16(a)
    b_hi, b_lo = split_bf16(b)
    eq = "bij,bjk->bik"
    out = jnp.einsum(eq, a_hi, b_hi, preferred_element_type=jnp.float32)
    out = out + jnp.einsum(eq, a_lo, b_hi, preferred_element_type=jnp.float32)
    return out + jnp.einsum(eq, a_hi, b_lo, preferred_element_type=jnp.float32)


def diag_kernel(t_hbm, o_ref, sems):
    nb = o_ref.shape[0]
    copies = [
        pltpu.make_async_copy(
            t_hbm.at[pl.ds(j * BLOCK, BLOCK), pl.ds(j * BLOCK, BLOCK)], o_ref.at[j], sems.at[j]
        )
        for j in range(nb)
    ]
    for one in copies:
        one.start()
    for one in copies:
        one.wait()


def prepare(tile):
    n = tile.shape[0]
    nb = n // BLOCK
    blocks = pl.pallas_call(
        diag_kernel,
        in_specs=[pl.BlockSpec(memory_space=pl.ANY)],
        out_specs=pl.BlockSpec(memory_space=pltpu.VMEM),
        out_shape=jax.ShapeDtypeStruct((nb, BLOCK, BLOCK), tile.dtype),
        scratch_shapes=[pltpu.SemaphoreType.DMA((nb,))],
    )(tile).astype(jnp.float32)
    eye = jnp.eye(BLOCK, dtype=jnp.float32)
    diag = jnp.sum(blocks * eye[None], axis=2)
    lower = jnp.tril(jnp.ones((BLOCK, BLOCK), jnp.bool_), -1)
    nil = jnp.where(lower[None], blocks / diag[:, :, None], 0.0)
    prod = eye[None] - nil
    power = nil
    steps = 1
    while 2 ** steps < BLOCK:
        power = mm3(power, power)
        prod = mm3(prod, eye[None] + power)
        steps += 1
    return prod, 1.0 / diag


def solve_kernel(f_ref, p_ref, d_ref, r_ref, o_ref, rest_ref):
    nb = p_ref.shape[0]
    rest_ref[...] = r_ref[...]

    def body(i, carry):
        j = nb - 1 - i
        start = pl.multiple_of(j * BLOCK, BLOCK)
        r_hi, r_lo = split_bf16(rest_ref[:, pl.ds(start, BLOCK)])
        p_hi, p_lo = split_bf16(p_ref[j])
        v = jnp.dot(r_hi, p_hi, preferred_element_type=jnp.float32)
        v = v + jnp.dot(r_lo, p_hi, preferred_element_type=jnp.float32)
        v = v + jnp.dot(r_hi, p_lo, preferred_element_type=jnp.float32)
        v = v * d_ref[pl.ds(j, 1), :]
        v_hi, v_lo = split_bf16(v)
        rows = f_ref[pl.ds(start, BLOCK), : rest_ref.shape[1]]
        upd = jnp.dot(v_hi, rows, preferred_element_type=jnp.float32)
        upd = upd + jnp.dot(v_lo, rows, preferred_element_type=jnp.float32)
        rest_ref[...] = rest_ref[...] - upd
        o_ref[:, pl.ds(start, BLOCK)] = v.astype(o_ref.dtype)
        return carry

    lax.fori_loop(0, nb, body, 0)


def kernel_solve(tile, prod, inv_diag, rhs):
    n = rhs.shape[0]
    cols = rhs.shape[1]
    vmem = pl.BlockSpec(memory_space=pltpu.VMEM)
    out_t = pl.pallas_call(
        solve_kernel,
        out_shape=jax.ShapeDtypeStruct((cols, n), jnp.bfloat16),
        in_specs=[vmem, vmem, vmem, vmem],
        out_specs=vmem,
        scratch_shapes=[pltpu.VMEM((cols, n), jnp.float32)],
        compiler_params=pltpu.CompilerParams(vmem_limit_bytes=48 * 1024 * 1024),
    )(tile, prod, inv_diag, rhs.T)
    return out_t.T


def chunked_permute(x, axis, perm, parts=4):
    pieces = jnp.split(x, parts, axis=0)
    return jnp.concatenate([lax.ppermute(p, axis, perm) for p in pieces], axis=0)


def ancestor_values(solved, owners, indices, counts):
    row_count = lax.axis_size("row")
    col_count = lax.axis_size("col")
    tiles_block = row_count * col_count
    row_index = lax.axis_index("row")
    col_index = lax.axis_index("col")
    tile_rows = indices.shape[1]
    columns = solved.shape[1]
    self_id = row_index * col_count + col_index
    owner_grid = owners.reshape(row_count, tiles_block)
    mine = (owner_grid == self_id).astype(jnp.int32)
    position = jnp.sum(mine * jnp.arange(tiles_block, dtype=jnp.int32)[None, :], axis=1)
    tile_ids = jnp.arange(row_count, dtype=jnp.int32) * tiles_block + position
    local_rows = indices[tile_ids]
    live_rows = jnp.arange(tile_rows, dtype=jnp.int32)[None, :] < counts[tile_ids][:, None]
    picked = solved[local_rows.reshape(-1)].reshape(row_count, tile_rows, columns)
    picked = jnp.where(live_rows[:, :, None], picked, jnp.zeros_like(picked))
    block_owners = lax.dynamic_slice_in_dim(owners, row_index * tiles_block, tiles_block)
    outgoing = jnp.broadcast_to(picked[:, None], (row_count, col_count, tile_rows, columns))
    outgoing = outgoing.reshape(row_count * col_count * tile_rows, columns)
    received = lax.all_to_all(outgoing, ("row", "col"), split_axis=0, concat_axis=0, tiled=True)
    slot_rows = received.reshape(tiles_block, tile_rows, columns)
    anc_values = slot_rows[block_owners].reshape(tiles_block * tile_rows, columns)
    return anc_values


def device_body(front, anc_weight, solved, owners, indices, counts, rhs_side):
    row_index = lax.axis_index("row")
    col_index = lax.axis_index("col")
    shard_rows, width = front.shape
    w_rows = anc_weight.shape[0]
    fold = shard_rows // w_rows
    both = jnp.concatenate([front, anc_weight.reshape(shard_rows, width // fold)], axis=1)
    both = lax.all_gather(both, "xh", axis=0, tiled=True)
    both = lax.all_gather(both, "y", axis=0, tiled=True)
    anc_values = ancestor_values(solved, owners, indices, counts)
    both = lax.all_gather(both, "z", axis=0, tiled=True)
    front_tile = both
    weight_tile = both[:, width:].reshape(-1, w_rows, fold, width // fold).reshape(-1, width)
    anc_total = lax.dot_general(
        weight_tile, anc_values, (((0,), (0,)), ((), ())), preferred_element_type=jnp.float32
    )
    prod, inv_diag = prepare(front_tile)
    rhs_values = rhs_side.astype(jnp.float32)
    down = [(1, 0)]
    left = [(1, 0)]
    right = [(0, 1)]

    own_one = anc_total.astype(jnp.bfloat16)
    other_one = lax.ppermute(own_one, "row", [(0, 1)])
    reduced_one = rhs_values - own_one.astype(jnp.float32) - other_one.astype(jnp.float32)
    sol_one = kernel_solve(front_tile, prod, inv_diag, reduced_one)
    got_one = chunked_permute(sol_one, "col", left)
    sol_one = jnp.where(col_index == 1, sol_one, got_one)

    front_term = lax.dot_general(
        front_tile[:, :width], sol_one, (((0,), (0,)), ((), ())), preferred_element_type=jnp.float32
    )
    own_zero = (anc_total + front_term).astype(jnp.bfloat16)
    own_zero = jnp.where(row_index == 0, anc_total.astype(jnp.bfloat16), own_zero)
    other_zero = lax.ppermute(own_zero, "row", down)
    reduced_zero = rhs_values - own_zero.astype(jnp.float32) - other_zero.astype(jnp.float32)
    sol_zero = kernel_solve(front_tile, prod, inv_diag, reduced_zero)
    got_zero = chunked_permute(sol_zero, "col", right)
    sol_zero = jnp.where(col_index == 0, sol_zero, got_zero)
    return jnp.where(row_index == 1, sol_one, sol_zero)


def solution(mesh):
    dims = dict(mesh.shape)
    rhs_split = (dims["rhs"] // 8, 4, 2)
    sub = jax.sharding.Mesh(
        mesh.devices.reshape(dims["row"], dims["col"], *rhs_split), ("row", "col", "z", "y", "xh")
    )
    rhs = ("z", "y", "xh")
    placed = (
        P(("row",) + rhs, "col"),
        P(("row",) + rhs, "col"),
        P(("row", "col"), rhs),
        P(),
        P(),
        P(),
        P("row", rhs),
    )
    return jax.shard_map(
        device_body, mesh=sub, in_specs=placed, out_specs=P("row", rhs), check_vma=False
    )
```

```python
import jax
import jax.numpy as jnp
from jax import lax
from jax.sharding import PartitionSpec as P
from jax.experimental import pallas as pl
from jax.experimental.pallas import tpu as pltpu

BLOCK = 128


def split_bf16(x):
    hi = x.astype(jnp.bfloat16)
    return hi, (x - hi.astype(jnp.float32)).astype(jnp.bfloat16)


def mm3(a, b):
    a_hi, a_lo = split_bf16(a)
    b_hi, b_lo = split_bf16(b)
    eq = "bij,bjk->bik"
    out = jnp.einsum(eq, a_hi, b_hi, preferred_element_type=jnp.float32)
    out = out + jnp.einsum(eq, a_lo, b_hi, preferred_element_type=jnp.float32)
    return out + jnp.einsum(eq, a_hi, b_lo, preferred_element_type=jnp.float32)


def diag_kernel(left_hbm, right_hbm, o_ref, sems):
    nb = o_ref.shape[0]
    half = nb // 2
    copies = []
    for j in range(nb):
        src, col = (left_hbm, j) if j < half else (right_hbm, j - half)
        copies.append(
            pltpu.make_async_copy(
                src.at[pl.ds(j * BLOCK, BLOCK), pl.ds(col * BLOCK, BLOCK)], o_ref.at[j], sems.at[j]
            )
        )
    for one in copies:
        one.start()
    for one in copies:
        one.wait()


def prepare(left, right):
    n = left.shape[0]
    nb = n // BLOCK
    blocks = pl.pallas_call(
        diag_kernel,
        in_specs=[pl.BlockSpec(memory_space=pl.ANY)] * 2,
        out_specs=pl.BlockSpec(memory_space=pltpu.VMEM),
        out_shape=jax.ShapeDtypeStruct((nb, BLOCK, BLOCK), left.dtype),
        scratch_shapes=[pltpu.SemaphoreType.DMA((nb,))],
    )(left, right).astype(jnp.float32)
    eye = jnp.eye(BLOCK, dtype=jnp.float32)
    diag = jnp.sum(blocks * eye[None], axis=2)
    lower = jnp.tril(jnp.ones((BLOCK, BLOCK), jnp.bool_), -1)
    nil = jnp.where(lower[None], blocks / diag[:, :, None], 0.0)
    prod = eye[None] - nil
    power = nil
    steps = 1
    while 2 ** steps < BLOCK:
        power = mm3(power, power)
        prod = mm3(prod, eye[None] + power)
        steps += 1
    return prod, 1.0 / diag


def solve_kernel(fl_ref, fr_ref, p_ref, d_ref, r_ref, o_ref, rest_ref):
    nb = p_ref.shape[0]
    rest_ref[...] = r_ref[...]

    def body(i, carry):
        j = nb - 1 - i
        start = pl.multiple_of(j * BLOCK, BLOCK)
        r_hi, r_lo = split_bf16(rest_ref[:, pl.ds(start, BLOCK)])
        p_hi, p_lo = split_bf16(p_ref[j])
        v = jnp.dot(r_hi, p_hi, preferred_element_type=jnp.float32)
        v = v + jnp.dot(r_lo, p_hi, preferred_element_type=jnp.float32)
        v = v + jnp.dot(r_hi, p_lo, preferred_element_type=jnp.float32)
        v = v * d_ref[pl.ds(j, 1), :]
        v_hi, v_lo = split_bf16(v)
        half = rest_ref.shape[1] // 2
        for f_ref, cols in ((fl_ref, slice(0, half)), (fr_ref, slice(half, 2 * half))):
            rows = f_ref[pl.ds(start, BLOCK), :half]
            upd = jnp.dot(v_hi, rows, preferred_element_type=jnp.float32)
            upd = upd + jnp.dot(v_lo, rows, preferred_element_type=jnp.float32)
            rest_ref[:, cols] = rest_ref[:, cols] - upd
        o_ref[:, pl.ds(start, BLOCK)] = v.astype(o_ref.dtype)
        return carry

    lax.fori_loop(0, nb, body, 0)


def kernel_solve(left, right, prod, inv_diag, rhs):
    n = rhs.shape[0]
    cols = rhs.shape[1]
    vmem = pl.BlockSpec(memory_space=pltpu.VMEM)
    out_t = pl.pallas_call(
        solve_kernel,
        out_shape=jax.ShapeDtypeStruct((cols, n), jnp.bfloat16),
        in_specs=[vmem, vmem, vmem, vmem, vmem],
        out_specs=vmem,
        scratch_shapes=[pltpu.VMEM((cols, n), jnp.float32)],
        compiler_params=pltpu.CompilerParams(vmem_limit_bytes=48 * 1024 * 1024),
    )(left, right, prod, inv_diag, rhs.T)
    return out_t.T


def chunked_permute(x, axis, perm, parts=4):
    pieces = jnp.split(x, parts, axis=0)
    return jnp.concatenate([lax.ppermute(p, axis, perm) for p in pieces], axis=0)


def ancestor_values(solved, owners, indices, counts):
    row_count = lax.axis_size("row")
    col_count = lax.axis_size("col")
    tiles_block = row_count * col_count
    row_index = lax.axis_index("row")
    col_index = lax.axis_index("col")
    tile_rows = indices.shape[1]
    columns = solved.shape[1]
    self_id = row_index * col_count + col_index
    owner_grid = owners.reshape(row_count, tiles_block)
    mine = (owner_grid == self_id).astype(jnp.int32)
    position = jnp.sum(mine * jnp.arange(tiles_block, dtype=jnp.int32)[None, :], axis=1)
    tile_ids = jnp.arange(row_count, dtype=jnp.int32) * tiles_block + position
    local_rows = indices[tile_ids]
    live_rows = jnp.arange(tile_rows, dtype=jnp.int32)[None, :] < counts[tile_ids][:, None]
    picked = solved[local_rows.reshape(-1)].reshape(row_count, tile_rows, columns)
    picked = jnp.where(live_rows[:, :, None], picked, jnp.zeros_like(picked))
    block_owners = lax.dynamic_slice_in_dim(owners, row_index * tiles_block, tiles_block)
    outgoing = jnp.broadcast_to(picked[:, None], (row_count, col_count, tile_rows, columns))
    outgoing = outgoing.reshape(row_count * col_count * tile_rows, columns)
    received = lax.all_to_all(outgoing, ("row", "col"), split_axis=0, concat_axis=0, tiled=True)
    slot_rows = received.reshape(tiles_block, tile_rows, columns)
    anc_values = slot_rows[block_owners].reshape(tiles_block * tile_rows, columns)
    return anc_values


def device_body(front, anc_weight, solved, owners, indices, counts, rhs_side):
    row_index = lax.axis_index("row")
    col_index = lax.axis_index("col")
    shard_rows, width = front.shape
    half = width // 2
    w_rows = anc_weight.shape[0]
    fold = shard_rows // w_rows
    partner = lax.ppermute(front, "row", [(0, 1), (1, 0)])
    first_owner = row_index == col_index
    half_one = jnp.where(first_owner, front[:, half:], partner[:, :half])
    both = jnp.concatenate([half_one, anc_weight.reshape(shard_rows, width // fold)], axis=1)
    both = lax.all_gather(both, "xh", axis=0, tiled=True)
    both = lax.all_gather(both, "y", axis=0, tiled=True)
    anc_values = ancestor_values(solved, owners, indices, counts)
    both = lax.all_gather(both, "z", axis=0, tiled=True)
    weight_tile = both[:, half:].reshape(-1, w_rows, fold, width // fold).reshape(-1, width)
    crit_left = lax.ppermute(both[:, :half], ("row", "col"), [(2, 0), (1, 3)])
    crit_right = both
    anc_total = lax.dot_general(
        weight_tile, anc_values, (((0,), (0,)), ((), ())), preferred_element_type=jnp.float32
    )
    prod, inv_diag = prepare(crit_left, crit_right)

    second_owner = row_index == 1 - col_index
    half_two = jnp.where(second_owner, front[:, half:], partner[:, :half])
    half_two, _ = lax.optimization_barrier((half_two, both))
    half_two = lax.all_gather(half_two, ("z", "y", "xh"), axis=0, tiled=True)
    prod_left = lax.ppermute(half_two, ("row", "col"), [(0, 2), (3, 1)])
    prod_right = half_two

    rhs_values = rhs_side.astype(jnp.float32)
    down = [(1, 0)]
    left = [(1, 0)]
    right = [(0, 1)]

    own_one = anc_total.astype(jnp.bfloat16)
    other_one = lax.ppermute(own_one, "row", [(0, 1)])
    reduced_one = rhs_values - own_one.astype(jnp.float32) - other_one.astype(jnp.float32)
    sol_one = kernel_solve(crit_left, crit_right, prod, inv_diag, reduced_one)
    got_one = chunked_permute(sol_one, "col", left)
    sol_one = jnp.where(col_index == 1, sol_one, got_one)

    dims = (((0,), (0,)), ((), ()))
    front_term = jnp.concatenate(
        [
            lax.dot_general(prod_left, sol_one, dims, preferred_element_type=jnp.float32),
            lax.dot_general(prod_right, sol_one, dims, preferred_element_type=jnp.float32),
        ],
        axis=0,
    )
    own_zero = (anc_total + front_term).astype(jnp.bfloat16)
    own_zero = jnp.where(row_index == 0, anc_total.astype(jnp.bfloat16), own_zero)
    other_zero = lax.ppermute(own_zero, "row", down)
    reduced_zero = rhs_values - own_zero.astype(jnp.float32) - other_zero.astype(jnp.float32)
    sol_zero = kernel_solve(crit_left, crit_right, prod, inv_diag, reduced_zero)
    got_zero = chunked_permute(sol_zero, "col", right)
    sol_zero = jnp.where(col_index == 0, sol_zero, got_zero)
    return jnp.where(row_index == 1, sol_one, sol_zero)


def solution(mesh):
    dims = dict(mesh.shape)
    rhs_split = (dims["rhs"] // 8, 4, 2)
    sub = jax.sharding.Mesh(
        mesh.devices.reshape(dims["row"], dims["col"], *rhs_split), ("row", "col", "z", "y", "xh")
    )
    rhs = ("z", "y", "xh")
    placed = (
        P(("row",) + rhs, "col"),
        P(("row",) + rhs, "col"),
        P(("row", "col"), rhs),
        P(),
        P(),
        P(),
        P("row", rhs),
    )
    return jax.shard_map(
        device_body, mesh=sub, in_specs=placed, out_specs=P("row", rhs), check_vma=False
    )
```

```python
import jax
import jax.numpy as jnp
from jax import lax
from jax.sharding import PartitionSpec as P
from jax.experimental import pallas as pl
from jax.experimental.pallas import tpu as pltpu

BLOCK = 128


def split_bf16(x):
    hi = x.astype(jnp.bfloat16)
    return hi, (x - hi.astype(jnp.float32)).astype(jnp.bfloat16)


def mm3(a, b):
    a_hi, a_lo = split_bf16(a)
    b_hi, b_lo = split_bf16(b)
    eq = "bij,bjk->bik"
    out = jnp.einsum(eq, a_hi, b_hi, preferred_element_type=jnp.float32)
    out = out + jnp.einsum(eq, a_lo, b_hi, preferred_element_type=jnp.float32)
    return out + jnp.einsum(eq, a_hi, b_lo, preferred_element_type=jnp.float32)


def diag_kernel(left_hbm, right_hbm, o_ref, sems):
    nb = o_ref.shape[0]
    half = nb // 2
    copies = []
    for j in range(nb):
        src, col = (left_hbm, j) if j < half else (right_hbm, j - half)
        copies.append(
            pltpu.make_async_copy(
                src.at[pl.ds(j * BLOCK, BLOCK), pl.ds(col * BLOCK, BLOCK)], o_ref.at[j], sems.at[j]
            )
        )
    for one in copies:
        one.start()
    for one in copies:
        one.wait()


def prepare(left, right):
    n = left.shape[0]
    nb = n // BLOCK
    blocks = pl.pallas_call(
        diag_kernel,
        in_specs=[pl.BlockSpec(memory_space=pl.ANY)] * 2,
        out_specs=pl.BlockSpec(memory_space=pltpu.VMEM),
        out_shape=jax.ShapeDtypeStruct((nb, BLOCK, BLOCK), left.dtype),
        scratch_shapes=[pltpu.SemaphoreType.DMA((nb,))],
    )(left, right).astype(jnp.float32)
    eye = jnp.eye(BLOCK, dtype=jnp.float32)
    diag = jnp.sum(blocks * eye[None], axis=2)
    lower = jnp.tril(jnp.ones((BLOCK, BLOCK), jnp.bool_), -1)
    nil = jnp.where(lower[None], blocks / diag[:, :, None], 0.0)
    prod = eye[None] - nil
    power = nil
    steps = 1
    while 2 ** steps < BLOCK:
        power = mm3(power, power)
        prod = mm3(prod, eye[None] + power)
        steps += 1
    return prod, 1.0 / diag


def solve_kernel(fl_ref, fr_ref, p_ref, d_ref, r_ref, o_ref, rest_ref):
    nb = p_ref.shape[0]
    rest_ref[...] = r_ref[...]

    def body(i, carry):
        j = nb - 1 - i
        start = pl.multiple_of(j * BLOCK, BLOCK)
        r_hi, r_lo = split_bf16(rest_ref[:, pl.ds(start, BLOCK)])
        p_hi, p_lo = split_bf16(p_ref[j])
        v = jnp.dot(r_hi, p_hi, preferred_element_type=jnp.float32)
        v = v + jnp.dot(r_lo, p_hi, preferred_element_type=jnp.float32)
        v = v + jnp.dot(r_hi, p_lo, preferred_element_type=jnp.float32)
        v = v * d_ref[pl.ds(j, 1), :]
        v_hi, v_lo = split_bf16(v)
        half = rest_ref.shape[1] // 2
        for f_ref, cols in ((fl_ref, slice(0, half)), (fr_ref, slice(half, 2 * half))):
            rows = f_ref[pl.ds(start, BLOCK), :half]
            upd = jnp.dot(v_hi, rows, preferred_element_type=jnp.float32)
            upd = upd + jnp.dot(v_lo, rows, preferred_element_type=jnp.float32)
            rest_ref[:, cols] = rest_ref[:, cols] - upd
        o_ref[:, pl.ds(start, BLOCK)] = v.astype(o_ref.dtype)
        return carry

    lax.fori_loop(0, nb, body, 0)


def kernel_solve(left, right, prod, inv_diag, rhs):
    n = rhs.shape[0]
    cols = rhs.shape[1]
    vmem = pl.BlockSpec(memory_space=pltpu.VMEM)
    out_t = pl.pallas_call(
        solve_kernel,
        out_shape=jax.ShapeDtypeStruct((cols, n), jnp.bfloat16),
        in_specs=[vmem, vmem, vmem, vmem, vmem],
        out_specs=vmem,
        scratch_shapes=[pltpu.VMEM((cols, n), jnp.float32)],
        compiler_params=pltpu.CompilerParams(vmem_limit_bytes=48 * 1024 * 1024),
    )(left, right, prod, inv_diag, rhs.T)
    return out_t.T


def chunked_permute(x, axis, perm, parts=4):
    pieces = jnp.split(x, parts, axis=0)
    return jnp.concatenate([lax.ppermute(p, axis, perm) for p in pieces], axis=0)


def ancestor_values(solved, owners, indices, counts):
    row_count = lax.axis_size("row")
    col_count = lax.axis_size("col")
    tiles_block = row_count * col_count
    row_index = lax.axis_index("row")
    col_index = lax.axis_index("col")
    tile_rows = indices.shape[1]
    columns = solved.shape[1]
    self_id = row_index * col_count + col_index
    owner_grid = owners.reshape(row_count, tiles_block)
    mine = (owner_grid == self_id).astype(jnp.int32)
    position = jnp.sum(mine * jnp.arange(tiles_block, dtype=jnp.int32)[None, :], axis=1)
    tile_ids = jnp.arange(row_count, dtype=jnp.int32) * tiles_block + position
    local_rows = indices[tile_ids]
    live_rows = jnp.arange(tile_rows, dtype=jnp.int32)[None, :] < counts[tile_ids][:, None]
    picked = solved[local_rows.reshape(-1)].reshape(row_count, tile_rows, columns)
    picked = jnp.where(live_rows[:, :, None], picked, jnp.zeros_like(picked))
    block_owners = lax.dynamic_slice_in_dim(owners, row_index * tiles_block, tiles_block)
    outgoing = jnp.broadcast_to(picked[:, None], (row_count, col_count, tile_rows, columns))
    outgoing = outgoing.reshape(row_count * col_count * tile_rows, columns)
    received = lax.all_to_all(outgoing, ("row", "col"), split_axis=0, concat_axis=0, tiled=True)
    slot_rows = received.reshape(tiles_block, tile_rows, columns)
    anc_values = slot_rows[block_owners].reshape(tiles_block * tile_rows, columns)
    return anc_values


def device_body(front, anc_weight, solved, owners, indices, counts, rhs_side):
    row_index = lax.axis_index("row")
    col_index = lax.axis_index("col")
    shard_rows, width = front.shape
    half = width // 2
    w_rows = anc_weight.shape[0]
    fold = shard_rows // w_rows
    partner = lax.ppermute(front, "row", [(0, 1), (1, 0)])
    first_owner = row_index == col_index
    half_one = jnp.where(first_owner, front[:, half:], partner[:, :half])
    both = jnp.concatenate([half_one, anc_weight.reshape(shard_rows, width // fold)], axis=1)
    both = lax.all_gather(both, "xh", axis=0, tiled=True)
    both = lax.all_gather(both, "y", axis=0, tiled=True)
    anc_values = ancestor_values(solved, owners, indices, counts)
    both = lax.all_gather(both, "z", axis=0, tiled=True)
    weight_tile = both[:, half:].reshape(-1, w_rows, fold, width // fold).reshape(-1, width)
    crit_left = lax.ppermute(both, ("row", "col"), [(2, 0), (1, 3)])
    crit_right = both
    anc_total = lax.dot_general(
        weight_tile, anc_values, (((0,), (0,)), ((), ())), preferred_element_type=jnp.float32
    )
    prod, inv_diag = prepare(crit_left, crit_right)

    second_owner = row_index == 1 - col_index
    half_two = jnp.where(second_owner, front[:, half:], partner[:, :half])
    half_two = lax.all_gather(half_two, "xh", axis=0, tiled=True)
    half_two = lax.all_gather(half_two, "y", axis=0, tiled=True)
    half_two, _ = lax.optimization_barrier((half_two, both))
    half_two = lax.all_gather(half_two, "z", axis=0, tiled=True)

    rhs_values = rhs_side.astype(jnp.float32)
    down = [(1, 0)]
    left = [(1, 0)]
    right = [(0, 1)]

    own_one = anc_total.astype(jnp.bfloat16)
    other_one = lax.ppermute(own_one, "row", [(0, 1)])
    reduced_one = rhs_values - own_one.astype(jnp.float32) - other_one.astype(jnp.float32)
    sol_one = kernel_solve(crit_left, crit_right, prod, inv_diag, reduced_one)
    got_one = chunked_permute(sol_one, "col", left)
    half_two, got_one = lax.optimization_barrier((half_two, got_one))
    sol_one = jnp.where(col_index == 1, sol_one, got_one)
    prod_left = lax.ppermute(half_two, ("row", "col"), [(0, 2), (3, 1)])
    prod_right = half_two

    dims = (((0,), (0,)), ((), ()))
    front_term = jnp.concatenate(
        [
            lax.dot_general(prod_left, sol_one, dims, preferred_element_type=jnp.float32),
            lax.dot_general(prod_right, sol_one, dims, preferred_element_type=jnp.float32),
        ],
        axis=0,
    )
    own_zero = (anc_total + front_term).astype(jnp.bfloat16)
    own_zero = jnp.where(row_index == 0, anc_total.astype(jnp.bfloat16), own_zero)
    other_zero = lax.ppermute(own_zero, "row", down)
    reduced_zero = rhs_values - own_zero.astype(jnp.float32) - other_zero.astype(jnp.float32)
    sol_zero = kernel_solve(crit_left, crit_right, prod, inv_diag, reduced_zero)
    got_zero = chunked_permute(sol_zero, "col", right)
    sol_zero = jnp.where(col_index == 0, sol_zero, got_zero)
    return jnp.where(row_index == 1, sol_one, sol_zero)


def solution(mesh):
    dims = dict(mesh.shape)
    rhs_split = (dims["rhs"] // 8, 4, 2)
    sub = jax.sharding.Mesh(
        mesh.devices.reshape(dims["row"], dims["col"], *rhs_split), ("row", "col", "z", "y", "xh")
    )
    rhs = ("z", "y", "xh")
    placed = (
        P(("row",) + rhs, "col"),
        P(("row",) + rhs, "col"),
        P(("row", "col"), rhs),
        P(),
        P(),
        P(),
        P("row", rhs),
    )
    return jax.shard_map(
        device_body, mesh=sub, in_specs=placed, out_specs=P("row", rhs), check_vma=False
    )
```

```python
import jax
import jax.numpy as jnp
from jax import lax
from jax.sharding import PartitionSpec as P
from jax.experimental import pallas as pl
from jax.experimental.pallas import tpu as pltpu

BLOCK = 128


def split_bf16(x):
    hi = x.astype(jnp.bfloat16)
    return hi, (x - hi.astype(jnp.float32)).astype(jnp.bfloat16)


def mm3(a, b):
    a_hi, a_lo = split_bf16(a)
    b_hi, b_lo = split_bf16(b)
    eq = "bij,bjk->bik"
    out = jnp.einsum(eq, a_hi, b_hi, preferred_element_type=jnp.float32)
    out = out + jnp.einsum(eq, a_lo, b_hi, preferred_element_type=jnp.float32)
    return out + jnp.einsum(eq, a_hi, b_lo, preferred_element_type=jnp.float32)


def diag_kernel(left_hbm, right_hbm, o_ref, sems):
    nb = o_ref.shape[0]
    half = nb // 2
    copies = []
    for j in range(nb):
        src, col = (left_hbm, j) if j < half else (right_hbm, j - half)
        copies.append(
            pltpu.make_async_copy(
                src.at[pl.ds(j * BLOCK, BLOCK), pl.ds(col * BLOCK, BLOCK)], o_ref.at[j], sems.at[j]
            )
        )
    for one in copies:
        one.start()
    for one in copies:
        one.wait()


def prepare(left, right):
    n = left.shape[0]
    nb = n // BLOCK
    blocks = pl.pallas_call(
        diag_kernel,
        in_specs=[pl.BlockSpec(memory_space=pl.ANY)] * 2,
        out_specs=pl.BlockSpec(memory_space=pltpu.VMEM),
        out_shape=jax.ShapeDtypeStruct((nb, BLOCK, BLOCK), left.dtype),
        scratch_shapes=[pltpu.SemaphoreType.DMA((nb,))],
    )(left, right).astype(jnp.float32)
    eye = jnp.eye(BLOCK, dtype=jnp.float32)
    diag = jnp.sum(blocks * eye[None], axis=2)
    lower = jnp.tril(jnp.ones((BLOCK, BLOCK), jnp.bool_), -1)
    nil = jnp.where(lower[None], blocks / diag[:, :, None], 0.0)
    prod = eye[None] - nil
    power = nil
    steps = 1
    while 2 ** steps < BLOCK:
        power = mm3(power, power)
        prod = mm3(prod, eye[None] + power)
        steps += 1
    return prod, 1.0 / diag


def solve_kernel(fl_ref, fr_ref, p_ref, d_ref, r_ref, o_ref, rest_ref):
    nb = p_ref.shape[0]
    rest_ref[...] = r_ref[...]

    def body(i, carry):
        j = nb - 1 - i
        start = pl.multiple_of(j * BLOCK, BLOCK)
        r_hi, r_lo = split_bf16(rest_ref[:, pl.ds(start, BLOCK)])
        p_hi, p_lo = split_bf16(p_ref[j])
        v = jnp.dot(r_hi, p_hi, preferred_element_type=jnp.float32)
        v = v + jnp.dot(r_lo, p_hi, preferred_element_type=jnp.float32)
        v = v + jnp.dot(r_hi, p_lo, preferred_element_type=jnp.float32)
        v = v * d_ref[pl.ds(j, 1), :]
        v_hi, v_lo = split_bf16(v)
        half = rest_ref.shape[1] // 2
        for f_ref, cols in ((fl_ref, slice(0, half)), (fr_ref, slice(half, 2 * half))):
            rows = f_ref[pl.ds(start, BLOCK), :half]
            upd = jnp.dot(v_hi, rows, preferred_element_type=jnp.float32)
            upd = upd + jnp.dot(v_lo, rows, preferred_element_type=jnp.float32)
            rest_ref[:, cols] = rest_ref[:, cols] - upd
        o_ref[:, pl.ds(start, BLOCK)] = v.astype(o_ref.dtype)
        return carry

    lax.fori_loop(0, nb, body, 0)


def kernel_solve(left, right, prod, inv_diag, rhs):
    n = rhs.shape[0]
    cols = rhs.shape[1]
    vmem = pl.BlockSpec(memory_space=pltpu.VMEM)
    out_t = pl.pallas_call(
        solve_kernel,
        out_shape=jax.ShapeDtypeStruct((cols, n), jnp.bfloat16),
        in_specs=[vmem, vmem, vmem, vmem, vmem],
        out_specs=vmem,
        scratch_shapes=[pltpu.VMEM((cols, n), jnp.float32)],
        compiler_params=pltpu.CompilerParams(vmem_limit_bytes=48 * 1024 * 1024),
    )(left, right, prod, inv_diag, rhs.T)
    return out_t.T


def ancestor_values(solved, owners, indices, counts):
    row_count = lax.axis_size("row")
    col_count = lax.axis_size("col")
    tiles_block = row_count * col_count
    row_index = lax.axis_index("row")
    col_index = lax.axis_index("col")
    tile_rows = indices.shape[1]
    columns = solved.shape[1]
    self_id = row_index * col_count + col_index
    owner_grid = owners.reshape(row_count, tiles_block)
    mine = (owner_grid == self_id).astype(jnp.int32)
    position = jnp.sum(mine * jnp.arange(tiles_block, dtype=jnp.int32)[None, :], axis=1)
    tile_ids = jnp.arange(row_count, dtype=jnp.int32) * tiles_block + position
    local_rows = indices[tile_ids]
    live_rows = jnp.arange(tile_rows, dtype=jnp.int32)[None, :] < counts[tile_ids][:, None]
    picked = solved[local_rows.reshape(-1)].reshape(row_count, tile_rows, columns)
    picked = jnp.where(live_rows[:, :, None], picked, jnp.zeros_like(picked))
    block_owners = lax.dynamic_slice_in_dim(owners, row_index * tiles_block, tiles_block)
    outgoing = jnp.broadcast_to(picked[:, None], (row_count, col_count, tile_rows, columns))
    outgoing = outgoing.reshape(row_count * col_count * tile_rows, columns)
    received = lax.all_to_all(outgoing, ("row", "col"), split_axis=0, concat_axis=0, tiled=True)
    slot_rows = received.reshape(tiles_block, tile_rows, columns)
    anc_values = slot_rows[block_owners].reshape(tiles_block * tile_rows, columns)
    return anc_values


def device_body(front, anc_weight, solved, owners, indices, counts, rhs_side):
    row_index = lax.axis_index("row")
    col_index = lax.axis_index("col")
    shard_rows, width = front.shape
    half = width // 2
    w_rows = anc_weight.shape[0]
    fold = shard_rows // w_rows
    partner = lax.ppermute(front, "row", [(0, 1), (1, 0)])
    first_owner = row_index == col_index
    half_one = jnp.where(first_owner, front[:, half:], partner[:, :half])
    both = jnp.concatenate([half_one, anc_weight.reshape(shard_rows, width // fold)], axis=1)
    both = lax.all_gather(both, "xh", axis=0, tiled=True)
    both = lax.all_gather(both, "y", axis=0, tiled=True)
    anc_values = ancestor_values(solved, owners, indices, counts)
    both = lax.all_gather(both, "z", axis=0, tiled=True)
    weight_tile = both[:, half:].reshape(-1, w_rows, fold, width // fold).reshape(-1, width)
    crit_left = lax.ppermute(both, ("row", "col"), [(2, 0), (1, 3)])
    crit_right = both
    anc_total = lax.dot_general(
        weight_tile, anc_values, (((0,), (0,)), ((), ())), preferred_element_type=jnp.float32
    )
    prod, inv_diag = prepare(crit_left, crit_right)

    second_owner = row_index == 1 - col_index
    half_two = jnp.where(second_owner, front[:, half:], partner[:, :half])
    half_two = lax.all_gather(half_two, "xh", axis=0, tiled=True)
    half_two = lax.all_gather(half_two, "y", axis=0, tiled=True)
    half_two, _ = lax.optimization_barrier((half_two, both))
    half_two = lax.all_gather(half_two, "z", axis=0, tiled=True)

    rhs_values = rhs_side.astype(jnp.float32)
    down = [(1, 0)]
    left = [(1, 0)]
    right = [(0, 1)]

    own_one = anc_total.astype(jnp.bfloat16)
    other_one = lax.ppermute(own_one, "row", [(0, 1)])
    reduced_one = rhs_values - own_one.astype(jnp.float32) - other_one.astype(jnp.float32)
    sol_one = kernel_solve(crit_left, crit_right, prod, inv_diag, reduced_one)
    got_one = lax.ppermute(sol_one, "col", left)
    half_two, got_one = lax.optimization_barrier((half_two, got_one))
    sol_one = jnp.where(col_index == 1, sol_one, got_one)
    prod_left = lax.ppermute(half_two, ("row", "col"), [(0, 2), (3, 1)])
    prod_right = half_two

    dims = (((0,), (0,)), ((), ()))
    front_term = jnp.concatenate(
        [
            lax.dot_general(prod_left, sol_one, dims, preferred_element_type=jnp.float32),
            lax.dot_general(prod_right, sol_one, dims, preferred_element_type=jnp.float32),
        ],
        axis=0,
    )
    own_zero = (anc_total + front_term).astype(jnp.bfloat16)
    own_zero = jnp.where(row_index == 0, anc_total.astype(jnp.bfloat16), own_zero)
    other_zero = lax.ppermute(own_zero, "row", down)
    reduced_zero = rhs_values - own_zero.astype(jnp.float32) - other_zero.astype(jnp.float32)
    sol_zero = kernel_solve(crit_left, crit_right, prod, inv_diag, reduced_zero)
    got_zero = lax.ppermute(sol_zero, "col", right)
    sol_zero = jnp.where(col_index == 0, sol_zero, got_zero)
    return jnp.where(row_index == 1, sol_one, sol_zero)


def solution(mesh):
    dims = dict(mesh.shape)
    rhs_split = (dims["rhs"] // 8, 4, 2)
    sub = jax.sharding.Mesh(
        mesh.devices.reshape(dims["row"], dims["col"], *rhs_split), ("row", "col", "z", "y", "xh")
    )
    rhs = ("z", "y", "xh")
    placed = (
        P(("row",) + rhs, "col"),
        P(("row",) + rhs, "col"),
        P(("row", "col"), rhs),
        P(),
        P(),
        P(),
        P("row", rhs),
    )
    return jax.shard_map(
        device_body, mesh=sub, in_specs=placed, out_specs=P("row", rhs), check_vma=False
    )
```
